128 devices in a mesh: sect: 4 (over y), blk: 32 (over x, z, core).
Axes of the slice: x: 4, y: 4, z: 4, core: 2. Of those that a mesh axis runs over, the one named last changes fastest.
Arguments:
- theta: bfloat16 [4, 4096, 2048], P('sect', 'blk'), may hold values from -6 to 6
- left_env: bfloat16 [4, 8, 4096, 4096], P('sect', None, 'blk'), may hold values from -0.125 to 0.125
- sector_ids: int32 [4, 4096], P('sect'), may hold values from 0 to 15, never falling along the last dimension, each value on 1 to 2560 neighbouring positions
- local_ops: float32 [4, 8, 16, 16], P('sect'), may hold values from -0.5 to 0.5
- edge_env: float32 [128, 128], replicated, may hold values from -0.5 to 0.5
Outputs:
- updated: bfloat16 [4, 4096, 2048], P('sect', 'blk')
- outgoing: float32 [4, 128, 128], P('sect')
The draws below stay inside these ranges and needn't reach their ends.
Inputs may be any that keep to these rules, and one draw needn't show every extreme that they name: `sector_ids`: within each section the sector numbers never fall along the rows; each sector holds 1 to 2560 rows and one holds exactly 2560.
All inputs are finite; a program needn't handle non-finite values.
Results may differ from the reference program's by a relative error of at most 0.00165.
Values may be sent and summed in bfloat16 or wider, within the bound.
No kernel may reach another device: no remote copies, remote signals or barrier semaphores. Data moves between devices by JAX's collectives and lax.ppermute only.
A program may use at most 128 MiB of HBM per device.

```python
import math
import jax
import jax.numpy as jnp
import numpy as np
from jax import lax

D = 4096
W = 8
P2 = 16
NSEC = 16
CW = 128
MOST = 2560
N_SECT = 4


def steps_of(stream_key, dims, shards, smallest, top_value):
    loudness, own = 1.0, jax.random.fold_in(stream_key, 6)
    for position, blocks in shards:
        steps = jnp.exp(jax.random.uniform(jax.random.fold_in(own, position), (blocks,), jnp.float32, smallest / len(shards), top_value / len(shards)))
        loudness = loudness * jnp.repeat(steps, dims[position] // blocks).reshape([-1 if axis == position else 1 for axis in range(len(dims))])
    return loudness


def length_profile(number_of, total, limit, slope):
    weights = [(1 << 20) // math.isqrt(rank ** slope) + 1 for rank in range(2, number_of + 1)]
    surplus, holding = total - limit - (number_of - 1), [1] * (number_of - 1)
    while surplus > 0:
        candidates = [i for i in range(number_of - 1) if holding[i] < limit]
        pool, left = sum([weights[i] for i in candidates]), surplus
        for i in candidates:
            extra = min(limit - holding[i], max(1, left * weights[i] // pool), surplus)
            holding[i] = holding[i] + extra
            surplus = surplus - extra
    return np.array([limit] + holding)


def ragged(own_key, number_of, total, reach, lean):
    if number_of == 2:
        one = jax.random.randint(own_key, (), max(1, total - reach), min(reach, total - 1) + 1)
        return jnp.stack([one, total - one])
    sizes = jnp.asarray(length_profile(number_of, total, reach, lean), jnp.int32)
    couples = (number_of - 1) // 2
    giver, taker = sizes[1:1 + 2 * couples:2], sizes[2:2 + 2 * couples:2]
    margin = jnp.minimum(giver - 1, reach - taker)
    passed = jax.random.randint(jax.random.fold_in(own_key, 1), (couples,), 0, 1 << 20) % (margin + 1)
    sizes = sizes.at[1:1 + 2 * couples:2].set(giver - passed).at[2:2 + 2 * couples:2].set(taker + passed)
    return sizes[jax.random.permutation(jax.random.fold_in(own_key, 2), number_of)]


def noise(own_key, shape, deviation, bound, cuts=(), held_as=jnp.bfloat16):
    gain = steps_of(own_key, shape, cuts, -0.22, 0.18) if cuts else 1.0
    drawn = jax.random.normal(own_key, shape, jnp.float32) * deviation * gain
    return jnp.minimum(jnp.maximum(drawn, -bound), bound).astype(held_as)


def setup_inputs(seed: int = 0) -> dict:
    seeds = jax.random.split(jax.random.key(seed), 6)
    theta = noise(seeds[0], (N_SECT, D, P2 * CW), 1.0, 6.0, ((0, 4), (1, 32)))
    left_env = noise(seeds[1], (N_SECT, W, D, D), MOST ** -0.5, 0.125, ((0, 4), (2, 32)))
    sector_ids = jax.vmap(lambda own: jnp.searchsorted(jnp.cumsum(ragged(own, NSEC, D, MOST, 2)), jnp.arange(D), side="right"))(jax.random.split(seeds[2], N_SECT)).reshape((N_SECT, D)).astype(jnp.int32)
    local_ops = noise(seeds[3], (N_SECT, W, P2, P2), (W * P2) ** -0.5, 0.5, ((0, 4),), jnp.float32)
    edge_env = noise(seeds[4], (CW, CW), CW ** -0.5, 0.5, (), jnp.float32)
    return {"theta": theta, "left_env": left_env, "sector_ids": sector_ids, "local_ops": local_ops, "edge_env": edge_env}


def one_section(theta_s, env_s, sec_s, ops_s):
    same = sec_s[:, None] == sec_s[None, :]
    theta_f = theta_s.astype(jnp.float32)

    def apply_one(env_w):
        masked = jnp.where(same, env_w, jnp.zeros_like(env_w)).astype(jnp.float32)
        return jnp.dot(masked, theta_f, precision=lax.Precision.HIGHEST)
    applied = lax.map(apply_one, env_s)
    applied = applied.reshape(W, D, P2, CW)
    acted = jnp.einsum('wpq,wiqc->ipc', ops_s, applied, precision=lax.Precision.HIGHEST)
    intersection = jnp.einsum('ipc,ipd->cd', theta_f.reshape(D, P2, CW), acted, precision=lax.Precision.HIGHEST)
    transfer = intersection * jnp.sqrt(jnp.float32(CW)) / jnp.sqrt(jnp.sum(intersection * intersection) + 1e-06)
    return (acted, transfer)

def reference(theta, left_env, sector_ids, local_ops, edge_env):
    incoming = edge_env
    updated = []
    outgoing = []
    for sect_no in range(N_SECT):
        acted, transfer = one_section(theta[sect_no], left_env[sect_no], sector_ids[sect_no], local_ops[sect_no])
        result = jnp.einsum('ipc,cd->ipd', acted, incoming, precision=lax.Precision.HIGHEST)
        updated.append(result.reshape(D, P2 * CW).astype(jnp.bfloat16))
        leaving = jnp.dot(incoming, transfer, precision=lax.Precision.HIGHEST)
        outgoing.append(leaving)
        incoming = leaving
    return (jnp.stack(updated), jnp.stack(outgoing))
```

```python
import jax
import jax.numpy as jnp
from jax import lax
from jax.sharding import PartitionSpec as P


def matprod(first, second):
    return jnp.dot(first, second, precision=lax.Precision.HIGHEST)


def butterfly_sum(value, axis):
    peers = lax.axis_size(axis)
    step = 1
    while step < peers:
        pairs = [(i, i ^ step) for i in range(peers)]
        value = value + lax.ppermute(value, axis, pairs)
        step *= 2
    return value


def gather_all(value, axis):
    peers = lax.axis_size(axis)
    me = lax.axis_index(axis)
    parts = [value]
    for shift in range(1, peers):
        pairs = [(i, (i + shift) % peers) for i in range(peers)]
        parts.append(lax.ppermute(value, axis, pairs))
    stacked = jnp.stack(parts)
    order = (me - jnp.arange(peers)) % peers
    return jnp.zeros_like(stacked).at[order].set(stacked)


def per_device(theta, left_env, sector_ids, local_ops, edge_env):
    rows_dev = theta.shape[1]
    width = theta.shape[2]
    chain_w = left_env.shape[1]
    phys = local_ops.shape[2]
    cols = width // phys
    theta_loc = theta[0]
    env_loc = left_env[0]
    sec_all = sector_ids[0]
    ops_loc = local_ops[0]
    my_block = lax.axis_index("blk")
    row_start = my_block * rows_dev
    my_sec = lax.dynamic_slice_in_dim(sec_all, row_start, rows_dev, 0)
    same = my_sec[:, None] == sec_all[None, :]
    masked = jnp.where(same[None, :, :], env_loc, jnp.zeros_like(env_loc))
    applied = jnp.einsum(
        "wij,jx->wix",
        masked,
        lax.all_gather(theta_loc, "blk", axis=0, tiled=True),
        preferred_element_type=jnp.float32,
    )
    applied = applied.reshape(chain_w, rows_dev, phys, cols)
    acted = jnp.einsum("wpq,wiqc->ipc", ops_loc, applied, precision=lax.Precision.HIGHEST)
    theta_f = theta_loc.astype(jnp.float32).reshape(rows_dev, phys, cols)
    partial_intersection = jnp.einsum(
        "ipc,ipd->cd", theta_f, acted, precision=lax.Precision.HIGHEST
    )
    intersection = butterfly_sum(partial_intersection, "blk")
    transfer = (
        intersection
        * jnp.sqrt(jnp.float32(cols))
        / jnp.sqrt(jnp.sum(intersection * intersection) + 1e-06)
    )
    transfers = gather_all(transfer, "sect")
    sect_no = lax.axis_index("sect")
    prefix = [edge_env]
    for step_no in range(lax.axis_size("sect")):
        prefix.append(matprod(prefix[-1], transfers[step_no]))
    prefix = jnp.stack(prefix)
    incoming = prefix[sect_no]
    outgoing = prefix[sect_no + 1]
    result = jnp.einsum("ipc,cd->ipd", acted, incoming, precision=lax.Precision.HIGHEST)
    updated = result.reshape(1, rows_dev, width).astype(jnp.bfloat16)
    return (updated, outgoing[None])


def solution(mesh):
    placed = (
        P("sect", "blk", None),
        P("sect", None, "blk", None),
        P("sect", None),
        P("sect", None, None, None),
        P(),
    )
    return jax.shard_map(
        per_device,
        mesh=mesh,
        in_specs=placed,
        out_specs=(P("sect", "blk", None), P("sect", None, None)),
        check_vma=False,
    )
```

```python
import functools

import jax
import jax.numpy as jnp
from jax import lax
from jax.experimental import pallas as pl
from jax.experimental.pallas import tpu as pltpu
from jax.sharding import PartitionSpec as P

K_TILE = 512


def matprod(first, second):
    return jnp.dot(first, second, precision=lax.Precision.HIGHEST)


def butterfly_sum(value, axis):
    peers = lax.axis_size(axis)
    step = 1
    while step < peers:
        pairs = [(i, i ^ step) for i in range(peers)]
        value = value + lax.ppermute(value, axis, pairs)
        step *= 2
    return value


def gather_all(value, axis):
    peers = lax.axis_size(axis)
    me = lax.axis_index(axis)
    parts = [value]
    for shift in range(1, peers):
        pairs = [(i, (i + shift) % peers) for i in range(peers)]
        parts.append(lax.ppermute(value, axis, pairs))
    stacked = jnp.stack(parts)
    order = (me - jnp.arange(peers)) % peers
    return jnp.zeros_like(stacked).at[order].set(stacked)


def masked_apply_kernel(span_ref, env_ref, theta_ref, sec_j_ref, sec_i_ref, out_ref):
    step = pl.program_id(0)

    @pl.when(step == 0)
    def _():
        out_ref[...] = jnp.zeros_like(out_ref)

    @pl.when(span_ref[0] + step <= span_ref[1])
    def _():
        same = sec_i_ref[...] == sec_j_ref[...]
        block = theta_ref[...]
        for w in range(out_ref.shape[0]):
            env_w = jnp.where(same, env_ref[w], jnp.zeros_like(env_ref[w]))
            out_ref[w] += jnp.dot(env_w, block, preferred_element_type=jnp.float32)


def masked_apply(env_loc, theta_all, sec_all, my_sec):
    chain_w, rows_dev, depth = env_loc.shape
    width = theta_all.shape[1]
    tiles = depth // K_TILE
    first = jnp.sum((sec_all < my_sec[0]).astype(jnp.int32))
    last = jnp.sum((sec_all <= my_sec[-1]).astype(jnp.int32)) - 1
    span = jnp.stack([first // K_TILE, last // K_TILE]).astype(jnp.int32)

    def tile_of(step, span_ref):
        return jnp.minimum(span_ref[0] + step, span_ref[1])

    grid_spec = pltpu.PrefetchScalarGridSpec(
        num_scalar_prefetch=1,
        grid=(tiles,),
        in_specs=[
            pl.BlockSpec((chain_w, rows_dev, K_TILE), lambda k, s: (0, 0, tile_of(k, s))),
            pl.BlockSpec((K_TILE, width), lambda k, s: (tile_of(k, s), 0)),
            pl.BlockSpec((1, K_TILE), lambda k, s: (0, tile_of(k, s))),
            pl.BlockSpec((rows_dev, 1), lambda k, s: (0, 0)),
        ],
        out_specs=pl.BlockSpec((chain_w, rows_dev, width), lambda k, s: (0, 0, 0)),
    )
    return pl.pallas_call(
        masked_apply_kernel,
        grid_spec=grid_spec,
        out_shape=jax.ShapeDtypeStruct((chain_w, rows_dev, width), jnp.float32),
        compiler_params=pltpu.CompilerParams(
            dimension_semantics=("arbitrary",), vmem_limit_bytes=48 * 1024 * 1024
        ),
    )(span, env_loc, theta_all, sec_all.reshape(1, depth), my_sec.reshape(rows_dev, 1))


def per_device(theta, left_env, sector_ids, local_ops, edge_env):
    rows_dev = theta.shape[1]
    width = theta.shape[2]
    chain_w = left_env.shape[1]
    phys = local_ops.shape[2]
    cols = width // phys
    theta_loc = theta[0]
    env_loc = left_env[0]
    sec_all = sector_ids[0]
    ops_loc = local_ops[0]
    my_block = lax.axis_index("blk")
    row_start = my_block * rows_dev
    my_sec = lax.dynamic_slice_in_dim(sec_all, row_start, rows_dev, 0)
    theta_all = lax.all_gather(theta_loc, "blk", axis=0, tiled=True)
    applied = masked_apply(env_loc, theta_all, sec_all, my_sec)
    applied = applied.reshape(chain_w, rows_dev, phys, cols)
    acted = jnp.einsum("wpq,wiqc->ipc", ops_loc, applied, precision=lax.Precision.HIGH)
    theta_f = theta_loc.astype(jnp.float32).reshape(rows_dev, phys, cols)
    partial_intersection = jnp.einsum(
        "ipc,ipd->cd", theta_f, acted, precision=lax.Precision.HIGH
    )
    intersection = butterfly_sum(partial_intersection, "blk")
    transfer = (
        intersection
        * jnp.sqrt(jnp.float32(cols))
        / jnp.sqrt(jnp.sum(intersection * intersection) + 1e-06)
    )
    transfers = gather_all(transfer, "sect")
    sect_no = lax.axis_index("sect")
    prefix = [edge_env]
    for step_no in range(lax.axis_size("sect")):
        prefix.append(matprod(prefix[-1], transfers[step_no]))
    prefix = jnp.stack(prefix)
    incoming = prefix[sect_no]
    outgoing = prefix[sect_no + 1]
    result = jnp.einsum("ipc,cd->ipd", acted, incoming, precision=lax.Precision.HIGH)
    updated = result.reshape(1, rows_dev, width).astype(jnp.bfloat16)
    return (updated, outgoing[None])


def solution(mesh):
    placed = (
        P("sect", "blk", None),
        P("sect", None, "blk", None),
        P("sect", None),
        P("sect", None, None, None),
        P(),
    )
    return jax.shard_map(
        per_device,
        mesh=mesh,
        in_specs=placed,
        out_specs=(P("sect", "blk", None), P("sect", None, None)),
        check_vma=False,
    )
```

```python
import functools

import jax
import jax.numpy as jnp
from jax import lax
from jax.experimental import pallas as pl
from jax.experimental.pallas import tpu as pltpu
from jax.sharding import PartitionSpec as P

K_TILE = 512


def matprod(first, second):
    return jnp.dot(first, second, precision=lax.Precision.HIGHEST)


def butterfly_sum(value, axis):
    peers = lax.axis_size(axis)
    step = 1
    while step < peers:
        pairs = [(i, i ^ step) for i in range(peers)]
        value = value + lax.ppermute(value, axis, pairs)
        step *= 2
    return value


def gather_all(value, axis):
    peers = lax.axis_size(axis)
    me = lax.axis_index(axis)
    parts = [value]
    for shift in range(1, peers):
        pairs = [(i, (i + shift) % peers) for i in range(peers)]
        parts.append(lax.ppermute(value, axis, pairs))
    stacked = jnp.stack(parts)
    order = (me - jnp.arange(peers)) % peers
    return jnp.zeros_like(stacked).at[order].set(stacked)


def masked_apply_kernel(span_ref, env_ref, theta_ref, sec_j_ref, sec_i_ref, out_ref):
    step = pl.program_id(0)

    @pl.when(step == 0)
    def _():
        out_ref[...] = jnp.zeros_like(out_ref)

    @pl.when(span_ref[0] + step <= span_ref[1])
    def _():
        same = sec_i_ref[...] == sec_j_ref[...]
        block = theta_ref[...]
        cols = out_ref.shape[2]
        phys = block.shape[1] // cols
        for w in range(env_ref.shape[0]):
            env_w = jnp.where(same, env_ref[w], jnp.zeros_like(env_ref[w]))
            part = jnp.dot(env_w, block, preferred_element_type=jnp.float32)
            for q in range(phys):
                out_ref[w * phys + q] += part[:, q * cols:(q + 1) * cols]


def masked_apply(env_loc, theta_all, sec_all, my_sec, phys):
    chain_w, rows_dev, depth = env_loc.shape
    width = theta_all.shape[1]
    tiles = depth // K_TILE
    first = jnp.sum((sec_all < my_sec[0]).astype(jnp.int32))
    last = jnp.sum((sec_all <= my_sec[-1]).astype(jnp.int32)) - 1
    span = jnp.stack([first // K_TILE, last // K_TILE]).astype(jnp.int32)

    def tile_of(step, span_ref):
        return jnp.minimum(span_ref[0] + step, span_ref[1])

    grid_spec = pltpu.PrefetchScalarGridSpec(
        num_scalar_prefetch=1,
        grid=(tiles,),
        in_specs=[
            pl.BlockSpec((chain_w, rows_dev, K_TILE), lambda k, s: (0, 0, tile_of(k, s))),
            pl.BlockSpec((K_TILE, width), lambda k, s: (tile_of(k, s), 0)),
            pl.BlockSpec((1, K_TILE), lambda k, s: (0, tile_of(k, s))),
            pl.BlockSpec((rows_dev, 1), lambda k, s: (0, 0)),
        ],
        out_specs=pl.BlockSpec((chain_w * phys, rows_dev, width // phys), lambda k, s: (0, 0, 0)),
    )
    return pl.pallas_call(
        masked_apply_kernel,
        grid_spec=grid_spec,
        out_shape=jax.ShapeDtypeStruct((chain_w * phys, rows_dev, width // phys), jnp.float32),
        compiler_params=pltpu.CompilerParams(
            dimension_semantics=("arbitrary",), vmem_limit_bytes=48 * 1024 * 1024
        ),
    )(span, env_loc, theta_all, sec_all.reshape(1, depth), my_sec.reshape(rows_dev, 1))


def per_device(theta, left_env, sector_ids, local_ops, edge_env):
    rows_dev = theta.shape[1]
    width = theta.shape[2]
    chain_w = left_env.shape[1]
    phys = local_ops.shape[2]
    cols = width // phys
    theta_loc = theta[0]
    env_loc = left_env[0]
    sec_all = sector_ids[0]
    ops_loc = local_ops[0]
    my_block = lax.axis_index("blk")
    row_start = my_block * rows_dev
    my_sec = lax.dynamic_slice_in_dim(sec_all, row_start, rows_dev, 0)
    theta_all = lax.all_gather(theta_loc, "blk", axis=0, tiled=True)
    applied = masked_apply(env_loc, theta_all, sec_all, my_sec, phys)
    applied = applied.reshape(chain_w, phys, rows_dev, cols)
    acted = jnp.einsum("wpq,wqic->ipc", ops_loc, applied, precision=lax.Precision.HIGH)
    theta_f = theta_loc.astype(jnp.float32).reshape(rows_dev, phys, cols)
    partial_intersection = jnp.einsum(
        "ipc,ipd->cd", theta_f, acted, precision=lax.Precision.HIGH
    )
    intersection = butterfly_sum(partial_intersection, "blk")
    transfer = (
        intersection
        * jnp.sqrt(jnp.float32(cols))
        / jnp.sqrt(jnp.sum(intersection * intersection) + 1e-06)
    )
    transfers = gather_all(transfer, "sect")
    sect_no = lax.axis_index("sect")
    prefix = [edge_env]
    for step_no in range(lax.axis_size("sect")):
        prefix.append(matprod(prefix[-1], transfers[step_no]))
    prefix = jnp.stack(prefix)
    incoming = prefix[sect_no]
    outgoing = prefix[sect_no + 1]
    result = jnp.einsum("ipc,cd->ipd", acted, incoming, precision=lax.Precision.HIGH)
    updated = result.reshape(1, rows_dev, width).astype(jnp.bfloat16)
    return (updated, outgoing[None])


def solution(mesh):
    placed = (
        P("sect", "blk", None),
        P("sect", None, "blk", None),
        P("sect", None),
        P("sect", None, None, None),
        P(),
    )
    return jax.shard_map(
        per_device,
        mesh=mesh,
        in_specs=placed,
        out_specs=(P("sect", "blk", None), P("sect", None, None)),
        check_vma=False,
    )
```

```python
import functools

import jax
import jax.numpy as jnp
from jax import lax
from jax.experimental import pallas as pl
from jax.experimental.pallas import tpu as pltpu
from jax.sharding import PartitionSpec as P

K_TILE = 256


def matprod(first, second):
    return jnp.dot(first, second, precision=lax.Precision.HIGHEST)


def butterfly_sum(value, axis):
    peers = lax.axis_size(axis)
    step = 1
    while step < peers:
        pairs = [(i, i ^ step) for i in range(peers)]
        value = value + lax.ppermute(value, axis, pairs)
        step *= 2
    return value


def gather_all(value, axis):
    peers = lax.axis_size(axis)
    me = lax.axis_index(axis)
    parts = [value]
    for shift in range(1, peers):
        pairs = [(i, (i + shift) % peers) for i in range(peers)]
        parts.append(lax.ppermute(value, axis, pairs))
    stacked = jnp.stack(parts)
    order = (me - jnp.arange(peers)) % peers
    return jnp.zeros_like(stacked).at[order].set(stacked)


def masked_apply_kernel(span_ref, env_ref, theta_ref, sec_j_ref, sec_i_ref, out_ref):
    step = pl.program_id(0)

    @pl.when(step == 0)
    def _():
        out_ref[...] = jnp.zeros_like(out_ref)

    @pl.when(span_ref[0] + step <= span_ref[1])
    def _():
        same = sec_i_ref[...] == sec_j_ref[...]
        block = theta_ref[...]
        for w in range(out_ref.shape[0]):
            env_w = jnp.where(same, env_ref[w], jnp.zeros_like(env_ref[w]))
            out_ref[w] += jnp.dot(env_w, block, preferred_element_type=jnp.float32)


def masked_apply(env_loc, theta_all, sec_all, my_sec):
    chain_w, rows_dev, depth = env_loc.shape
    width = theta_all.shape[1]
    tiles = depth // K_TILE
    first = jnp.sum((sec_all < my_sec[0]).astype(jnp.int32))
    last = jnp.sum((sec_all <= my_sec[-1]).astype(jnp.int32)) - 1
    span = jnp.stack([first // K_TILE, last // K_TILE]).astype(jnp.int32)

    def tile_of(step, span_ref):
        return jnp.minimum(span_ref[0] + step, span_ref[1])

    grid_spec = pltpu.PrefetchScalarGridSpec(
        num_scalar_prefetch=1,
        grid=(tiles,),
        in_specs=[
            pl.BlockSpec((chain_w, rows_dev, K_TILE), lambda k, s: (0, 0, tile_of(k, s))),
            pl.BlockSpec((K_TILE, width), lambda k, s: (tile_of(k, s), 0)),
            pl.BlockSpec((1, K_TILE), lambda k, s: (0, tile_of(k, s))),
            pl.BlockSpec((rows_dev, 1), lambda k, s: (0, 0)),
        ],
        out_specs=pl.BlockSpec((chain_w, rows_dev, width), lambda k, s: (0, 0, 0)),
    )
    return pl.pallas_call(
        masked_apply_kernel,
        grid_spec=grid_spec,
        out_shape=jax.ShapeDtypeStruct((chain_w, rows_dev, width), jnp.float32),
        compiler_params=pltpu.CompilerParams(
            dimension_semantics=("arbitrary",), vmem_limit_bytes=48 * 1024 * 1024
        ),
    )(span, env_loc, theta_all, sec_all.reshape(1, depth), my_sec.reshape(rows_dev, 1))


def per_device(theta, left_env, sector_ids, local_ops, edge_env):
    rows_dev = theta.shape[1]
    width = theta.shape[2]
    chain_w = left_env.shape[1]
    phys = local_ops.shape[2]
    cols = width // phys
    theta_loc = theta[0]
    env_loc = left_env[0]
    sec_all = sector_ids[0]
    ops_loc = local_ops[0]
    my_block = lax.axis_index("blk")
    row_start = my_block * rows_dev
    my_sec = lax.dynamic_slice_in_dim(sec_all, row_start, rows_dev, 0)
    theta_all = lax.all_gather(theta_loc, "blk", axis=0, tiled=True)
    applied = masked_apply(env_loc, theta_all, sec_all, my_sec)
    applied = applied.reshape(chain_w, rows_dev, phys, cols)
    acted = jnp.einsum("wpq,wiqc->ipc", ops_loc, applied, precision=lax.Precision.HIGH)
    theta_f = theta_loc.astype(jnp.float32).reshape(rows_dev, phys, cols)
    partial_intersection = jnp.einsum(
        "ipc,ipd->cd", theta_f, acted, precision=lax.Precision.HIGH
    )
    intersection = butterfly_sum(partial_intersection, "blk")
    transfer = (
        intersection
        * jnp.sqrt(jnp.float32(cols))
        / jnp.sqrt(jnp.sum(intersection * intersection) + 1e-06)
    )
    transfers = gather_all(transfer, "sect")
    sect_no = lax.axis_index("sect")
    prefix = [edge_env]
    for step_no in range(lax.axis_size("sect")):
        prefix.append(matprod(prefix[-1], transfers[step_no]))
    prefix = jnp.stack(prefix)
    incoming = prefix[sect_no]
    outgoing = prefix[sect_no + 1]
    result = jnp.einsum("ipc,cd->ipd", acted, incoming, precision=lax.Precision.HIGH)
    updated = result.reshape(1, rows_dev, width).astype(jnp.bfloat16)
    return (updated, outgoing[None])


def solution(mesh):
    placed = (
        P("sect", "blk", None),
        P("sect", None, "blk", None),
        P("sect", None),
        P("sect", None, None, None),
        P(),
    )
    return jax.shard_map(
        per_device,
        mesh=mesh,
        in_specs=placed,
        out_specs=(P("sect", "blk", None), P("sect", None, None)),
        check_vma=False,
    )
```

```python
import functools

import jax
import jax.numpy as jnp
from jax import lax
from jax.experimental import pallas as pl
from jax.experimental.pallas import tpu as pltpu
from jax.sharding import PartitionSpec as P

K_TILE = 256


def matprod(first, second):
    return jnp.dot(first, second, precision=lax.Precision.HIGHEST)


def butterfly_sum(value, axis):
    peers = lax.axis_size(axis)
    step = 1
    while step < peers:
        pairs = [(i, i ^ step) for i in range(peers)]
        value = value + lax.ppermute(value, axis, pairs)
        step *= 2
    return value


def gather_all(value, axis):
    peers = lax.axis_size(axis)
    me = lax.axis_index(axis)
    parts = [value]
    for shift in range(1, peers):
        pairs = [(i, (i + shift) % peers) for i in range(peers)]
        parts.append(lax.ppermute(value, axis, pairs))
    stacked = jnp.stack(parts)
    order = (me - jnp.arange(peers)) % peers
    return jnp.zeros_like(stacked).at[order].set(stacked)


def masked_apply_kernel(span_ref, env_ref, theta_ref, sec_j_ref, sec_i_ref, out_ref):
    step = pl.program_id(0)

    @pl.when(step == 0)
    def _():
        out_ref[...] = jnp.zeros_like(out_ref)

    @pl.when(span_ref[0] + step <= span_ref[1])
    def _():
        same = sec_i_ref[...] == sec_j_ref[...]
        block = theta_ref[...]
        cols = out_ref.shape[2]
        phys = block.shape[1] // cols
        for w in range(env_ref.shape[0]):
            env_w = jnp.where(same, env_ref[w], jnp.zeros_like(env_ref[w]))
            part = jnp.dot(env_w, block, preferred_element_type=jnp.float32)
            for q in range(phys):
                out_ref[w * phys + q] += part[:, q * cols:(q + 1) * cols]


def masked_apply(env_loc, theta_all, sec_all, my_sec, phys):
    chain_w, rows_dev, depth = env_loc.shape
    width = theta_all.shape[1]
    tiles = depth // K_TILE
    first = jnp.sum((sec_all < my_sec[0]).astype(jnp.int32))
    last = jnp.sum((sec_all <= my_sec[-1]).astype(jnp.int32)) - 1
    span = jnp.stack([first // K_TILE, last // K_TILE]).astype(jnp.int32)

    def tile_of(step, span_ref):
        return jnp.minimum(span_ref[0] + step, span_ref[1])

    grid_spec = pltpu.PrefetchScalarGridSpec(
        num_scalar_prefetch=1,
        grid=(tiles,),
        in_specs=[
            pl.BlockSpec((chain_w, rows_dev, K_TILE), lambda k, s: (0, 0, tile_of(k, s))),
            pl.BlockSpec((K_TILE, width), lambda k, s: (tile_of(k, s), 0)),
            pl.BlockSpec((1, K_TILE), lambda k, s: (0, tile_of(k, s))),
            pl.BlockSpec((rows_dev, 1), lambda k, s: (0, 0)),
        ],
        out_specs=pl.BlockSpec((chain_w * phys, rows_dev, width // phys), lambda k, s: (0, 0, 0)),
    )
    return pl.pallas_call(
        masked_apply_kernel,
        grid_spec=grid_spec,
        out_shape=jax.ShapeDtypeStruct((chain_w * phys, rows_dev, width // phys), jnp.float32),
        compiler_params=pltpu.CompilerParams(
            dimension_semantics=("arbitrary",), vmem_limit_bytes=48 * 1024 * 1024
        ),
    )(span, env_loc, theta_all, sec_all.reshape(1, depth), my_sec.reshape(rows_dev, 1))


def per_device(theta, left_env, sector_ids, local_ops, edge_env):
    rows_dev = theta.shape[1]
    width = theta.shape[2]
    chain_w = left_env.shape[1]
    phys = local_ops.shape[2]
    cols = width // phys
    theta_loc = theta[0]
    env_loc = left_env[0]
    sec_all = sector_ids[0]
    ops_loc = local_ops[0]
    my_block = lax.axis_index("blk")
    row_start = my_block * rows_dev
    my_sec = lax.dynamic_slice_in_dim(sec_all, row_start, rows_dev, 0)
    theta_all = lax.all_gather(theta_loc, "blk", axis=0, tiled=True)
    applied = masked_apply(env_loc, theta_all, sec_all, my_sec, phys)
    applied = applied.reshape(chain_w, phys, rows_dev, cols)
    theta_f = theta_loc.astype(jnp.float32).reshape(rows_dev, phys, cols)
    theta_ops = jnp.einsum("wpq,ipc->wqic", ops_loc, theta_f, precision=lax.Precision.HIGH)
    partial_intersection = jnp.einsum(
        "wqic,wqid->cd", theta_ops, applied, precision=lax.Precision.HIGH
    )
    acted = jnp.einsum("wpq,wqic->ipc", ops_loc, applied, precision=lax.Precision.HIGH)
    intersection = butterfly_sum(partial_intersection, "blk")
    transfer = (
        intersection
        * jnp.sqrt(jnp.float32(cols))
        / jnp.sqrt(jnp.sum(intersection * intersection) + 1e-06)
    )
    transfers = gather_all(transfer, "sect")
    sect_no = lax.axis_index("sect")
    prefix = [edge_env]
    for step_no in range(lax.axis_size("sect")):
        prefix.append(matprod(prefix[-1], transfers[step_no]))
    prefix = jnp.stack(prefix)
    incoming = prefix[sect_no]
    outgoing = prefix[sect_no + 1]
    result = jnp.einsum("ipc,cd->ipd", acted, incoming, precision=lax.Precision.HIGH)
    updated = result.reshape(1, rows_dev, width).astype(jnp.bfloat16)
    return (updated, outgoing[None])


def solution(mesh):
    placed = (
        P("sect", "blk", None),
        P("sect", None, "blk", None),
        P("sect", None),
        P("sect", None, None, None),
        P(),
    )
    return jax.shard_map(
        per_device,
        mesh=mesh,
        in_specs=placed,
        out_specs=(P("sect", "blk", None), P("sect", None, None)),
        check_vma=False,
    )
```

```python
import functools

import jax
import jax.numpy as jnp
from jax import lax
from jax.experimental import pallas as pl
from jax.experimental.pallas import tpu as pltpu
from jax.sharding import PartitionSpec as P

K_TILE = 256


def matprod(first, second):
    return jnp.dot(first, second, precision=lax.Precision.HIGHEST)


def butterfly_sum(value, axis):
    peers = lax.axis_size(axis)
    step = 1
    while step < peers:
        pairs = [(i, i ^ step) for i in range(peers)]
        value = value + lax.ppermute(value, axis, pairs)
        step *= 2
    return value


def gather_all(value, axis):
    peers = lax.axis_size(axis)
    me = lax.axis_index(axis)
    parts = [value]
    for shift in range(1, peers):
        pairs = [(i, (i + shift) % peers) for i in range(peers)]
        parts.append(lax.ppermute(value, axis, pairs))
    stacked = jnp.stack(parts)
    order = (me - jnp.arange(peers)) % peers
    return jnp.zeros_like(stacked).at[order].set(stacked)


def masked_apply_kernel(span_ref, env_ref, theta_ref, sec_j_ref, sec_i_ref, to_ref, out_ref, inter_ref):
    step = pl.program_id(0)

    @pl.when(step == 0)
    def _():
        out_ref[...] = jnp.zeros_like(out_ref)

    @pl.when(span_ref[0] + step <= span_ref[1])
    def _():
        same = sec_i_ref[...] == sec_j_ref[...]
        block = theta_ref[...]
        for w in range(out_ref.shape[0]):
            env_w = jnp.where(same, env_ref[w], jnp.zeros_like(env_ref[w]))
            out_ref[w] += jnp.dot(env_w, block, preferred_element_type=jnp.float32)

    @pl.when(step == pl.num_programs(0) - 1)
    def _():
        cols = inter_ref.shape[1]
        phys = out_ref.shape[2] // cols

        def one_w(w, acc):
            for q in range(phys):
                part = out_ref[w, :, q * cols:(q + 1) * cols]
                part_hi = part.astype(jnp.bfloat16)
                part_lo = (part - part_hi.astype(jnp.float32)).astype(jnp.bfloat16)
                t = to_ref[w, q * cols:(q + 1) * cols, :]
                t_hi = t.astype(jnp.bfloat16)
                t_lo = (t - t_hi.astype(jnp.float32)).astype(jnp.bfloat16)
                acc = acc + jnp.dot(t_hi, part_hi, preferred_element_type=jnp.float32)
                acc = acc + jnp.dot(t_hi, part_lo, preferred_element_type=jnp.float32)
                acc = acc + jnp.dot(t_lo, part_hi, preferred_element_type=jnp.float32)
            return acc

        inter_ref[...] = lax.fori_loop(
            0, out_ref.shape[0], one_w, jnp.zeros(inter_ref.shape, jnp.float32)
        )


def masked_apply(env_loc, theta_all, sec_all, my_sec, theta_ops, cols):
    chain_w, rows_dev, depth = env_loc.shape
    width = theta_all.shape[1]
    tiles = depth // K_TILE
    first = jnp.sum((sec_all < my_sec[0]).astype(jnp.int32))
    last = jnp.sum((sec_all <= my_sec[-1]).astype(jnp.int32)) - 1
    span = jnp.stack([first // K_TILE, last // K_TILE]).astype(jnp.int32)

    def tile_of(step, span_ref):
        return jnp.minimum(span_ref[0] + step, span_ref[1])

    grid_spec = pltpu.PrefetchScalarGridSpec(
        num_scalar_prefetch=1,
        grid=(tiles,),
        in_specs=[
            pl.BlockSpec((chain_w, rows_dev, K_TILE), lambda k, s: (0, 0, tile_of(k, s))),
            pl.BlockSpec((K_TILE, width), lambda k, s: (tile_of(k, s), 0)),
            pl.BlockSpec((1, K_TILE), lambda k, s: (0, tile_of(k, s))),
            pl.BlockSpec((rows_dev, 1), lambda k, s: (0, 0)),
            pl.BlockSpec((chain_w, width, rows_dev), lambda k, s: (0, 0, 0)),
        ],
        out_specs=[
            pl.BlockSpec((chain_w, rows_dev, width), lambda k, s: (0, 0, 0)),
            pl.BlockSpec((cols, cols), lambda k, s: (0, 0)),
        ],
    )
    return pl.pallas_call(
        masked_apply_kernel,
        grid_spec=grid_spec,
        out_shape=[
            jax.ShapeDtypeStruct((chain_w, rows_dev, width), jnp.float32),
            jax.ShapeDtypeStruct((cols, cols), jnp.float32),
        ],
        compiler_params=pltpu.CompilerParams(
            dimension_semantics=("arbitrary",), vmem_limit_bytes=56 * 1024 * 1024
        ),
    )(span, env_loc, theta_all, sec_all.reshape(1, depth), my_sec.reshape(rows_dev, 1), theta_ops)


def per_device(theta, left_env, sector_ids, local_ops, edge_env):
    rows_dev = theta.shape[1]
    width = theta.shape[2]
    chain_w = left_env.shape[1]
    phys = local_ops.shape[2]
    cols = width // phys
    theta_loc = theta[0]
    env_loc = left_env[0]
    sec_all = sector_ids[0]
    ops_loc = local_ops[0]
    my_block = lax.axis_index("blk")
    row_start = my_block * rows_dev
    my_sec = lax.dynamic_slice_in_dim(sec_all, row_start, rows_dev, 0)
    theta_all = lax.all_gather(theta_loc, "blk", axis=0, tiled=True)
    theta_f = theta_loc.astype(jnp.float32).reshape(rows_dev, phys, cols)
    theta_ops = jnp.einsum(
        "wpq,ipc->wqci", ops_loc, theta_f, precision=lax.Precision.HIGHEST
    ).reshape(chain_w, width, rows_dev)
    applied, partial_intersection = masked_apply(
        env_loc, theta_all, sec_all, my_sec, theta_ops, cols
    )
    applied = applied.reshape(chain_w, rows_dev, phys, cols)
    acted = jnp.einsum("wpq,wiqc->ipc", ops_loc, applied, precision=lax.Precision.HIGH)
    intersection = butterfly_sum(partial_intersection, "blk")
    transfer = (
        intersection
        * jnp.sqrt(jnp.float32(cols))
        / jnp.sqrt(jnp.sum(intersection * intersection) + 1e-06)
    )
    transfers = gather_all(transfer, "sect")
    sect_no = lax.axis_index("sect")
    prefix = [edge_env]
    for step_no in range(lax.axis_size("sect")):
        prefix.append(matprod(prefix[-1], transfers[step_no]))
    prefix = jnp.stack(prefix)
    incoming = prefix[sect_no]
    outgoing = prefix[sect_no + 1]
    result = jnp.einsum("ipc,cd->ipd", acted, incoming, precision=lax.Precision.HIGH)
    updated = result.reshape(1, rows_dev, width).astype(jnp.bfloat16)
    return (updated, outgoing[None])


def solution(mesh):
    placed = (
        P("sect", "blk", None),
        P("sect", None, "blk", None),
        P("sect", None),
        P("sect", None, None, None),
        P(),
    )
    return jax.shard_map(
        per_device,
        mesh=mesh,
        in_specs=placed,
        out_specs=(P("sect", "blk", None), P("sect", None, None)),
        check_vma=False,
    )
```

```python
import functools

import jax
import jax.numpy as jnp
from jax import lax
from jax.experimental import pallas as pl
from jax.experimental.pallas import tpu as pltpu
from jax.sharding import PartitionSpec as P

K_TILE = 256


def matprod(first, second):
    return jnp.dot(first, second, precision=lax.Precision.HIGHEST)


def butterfly_sum(value, axis):
    peers = lax.axis_size(axis)
    step = 1
    while step < peers:
        pairs = [(i, i ^ step) for i in range(peers)]
        value = value + lax.ppermute(value, axis, pairs)
        step *= 2
    return value


def gather_all(value, axis):
    peers = lax.axis_size(axis)
    me = lax.axis_index(axis)
    parts = [value]
    for shift in range(1, peers):
        pairs = [(i, (i + shift) % peers) for i in range(peers)]
        parts.append(lax.ppermute(value, axis, pairs))
    stacked = jnp.stack(parts)
    order = (me - jnp.arange(peers)) % peers
    return jnp.zeros_like(stacked).at[order].set(stacked)


def masked_apply_kernel(span_ref, env_ref, theta_ref, sec_j_ref, sec_i_ref, out_ref):
    step = pl.program_id(0)

    @pl.when(step == 0)
    def _():
        out_ref[...] = jnp.zeros_like(out_ref)

    @pl.when(span_ref[0] + step <= span_ref[1])
    def _():
        same = sec_i_ref[...] == sec_j_ref[...]
        env = env_ref[...]
        masked = jnp.where(same[None], env, jnp.zeros_like(env))
        masked = masked.reshape(out_ref.shape[0], env.shape[2])
        out_ref[...] += jnp.dot(masked, theta_ref[...], preferred_element_type=jnp.float32)


def masked_apply(env_loc, theta_all, sec_all, my_sec):
    chain_w, rows_dev, depth = env_loc.shape
    width = theta_all.shape[1]
    tiles = depth // K_TILE
    first = jnp.sum((sec_all < my_sec[0]).astype(jnp.int32))
    last = jnp.sum((sec_all <= my_sec[-1]).astype(jnp.int32)) - 1
    span = jnp.stack([first // K_TILE, last // K_TILE]).astype(jnp.int32)

    def tile_of(step, span_ref):
        return jnp.minimum(span_ref[0] + step, span_ref[1])

    grid_spec = pltpu.PrefetchScalarGridSpec(
        num_scalar_prefetch=1,
        grid=(tiles,),
        in_specs=[
            pl.BlockSpec((chain_w, rows_dev, K_TILE), lambda k, s: (0, 0, tile_of(k, s))),
            pl.BlockSpec((K_TILE, width), lambda k, s: (tile_of(k, s), 0)),
            pl.BlockSpec((1, K_TILE), lambda k, s: (0, tile_of(k, s))),
            pl.BlockSpec((rows_dev, 1), lambda k, s: (0, 0)),
        ],
        out_specs=pl.BlockSpec((chain_w * rows_dev, width), lambda k, s: (0, 0)),
    )
    return pl.pallas_call(
        masked_apply_kernel,
        grid_spec=grid_spec,
        out_shape=jax.ShapeDtypeStruct((chain_w * rows_dev, width), jnp.float32),
        compiler_params=pltpu.CompilerParams(
            dimension_semantics=("arbitrary",), vmem_limit_bytes=48 * 1024 * 1024
        ),
    )(span, env_loc, theta_all, sec_all.reshape(1, depth), my_sec.reshape(rows_dev, 1))


def per_device(theta, left_env, sector_ids, local_ops, edge_env):
    rows_dev = theta.shape[1]
    width = theta.shape[2]
    chain_w = left_env.shape[1]
    phys = local_ops.shape[2]
    cols = width // phys
    theta_loc = theta[0]
    env_loc = left_env[0]
    sec_all = sector_ids[0]
    ops_loc = local_ops[0]
    my_block = lax.axis_index("blk")
    row_start = my_block * rows_dev
    my_sec = lax.dynamic_slice_in_dim(sec_all, row_start, rows_dev, 0)
    theta_all = lax.all_gather(theta_loc, "blk", axis=0, tiled=True)
    applied = masked_apply(env_loc, theta_all, sec_all, my_sec)
    applied = applied.reshape(chain_w, rows_dev, phys, cols)
    acted = jnp.einsum("wpq,wiqc->ipc", ops_loc, applied, precision=lax.Precision.HIGH)
    theta_f = theta_loc.astype(jnp.float32).reshape(rows_dev, phys, cols)
    partial_intersection = jnp.einsum(
        "ipc,ipd->cd", theta_f, acted, precision=lax.Precision.HIGH
    )
    intersection = butterfly_sum(partial_intersection, "blk")
    transfer = (
        intersection
        * jnp.sqrt(jnp.float32(cols))
        / jnp.sqrt(jnp.sum(intersection * intersection) + 1e-06)
    )
    transfers = gather_all(transfer, "sect")
    sect_no = lax.axis_index("sect")
    prefix = [edge_env]
    for step_no in range(lax.axis_size("sect")):
        prefix.append(matprod(prefix[-1], transfers[step_no]))
    prefix = jnp.stack(prefix)
    incoming = prefix[sect_no]
    outgoing = prefix[sect_no + 1]
    result = jnp.einsum("ipc,cd->ipd", acted, incoming, precision=lax.Precision.HIGH)
    updated = result.reshape(1, rows_dev, width).astype(jnp.bfloat16)
    return (updated, outgoing[None])


def solution(mesh):
    placed = (
        P("sect", "blk", None),
        P("sect", None, "blk", None),
        P("sect", None),
        P("sect", None, None, None),
        P(),
    )
    return jax.shard_map(
        per_device,
        mesh=mesh,
        in_specs=placed,
        out_specs=(P("sect", "blk", None), P("sect", None, None)),
        check_vma=False,
    )
```

```python
import functools

import jax
import jax.numpy as jnp
from jax import lax
from jax.experimental import pallas as pl
from jax.experimental.pallas import tpu as pltpu
from jax.sharding import PartitionSpec as P

K_TILE = 256


def matprod(first, second):
    return jnp.dot(first, second, precision=lax.Precision.HIGHEST)


def butterfly_sum(value, axis):
    peers = lax.axis_size(axis)
    step = 1
    while step < peers:
        pairs = [(i, i ^ step) for i in range(peers)]
        value = value + lax.ppermute(value, axis, pairs)
        step *= 2
    return value


def gather_all(value, axis):
    peers = lax.axis_size(axis)
    me = lax.axis_index(axis)
    parts = [value]
    for shift in range(1, peers):
        pairs = [(i, (i + shift) % peers) for i in range(peers)]
        parts.append(lax.ppermute(value, axis, pairs))
    stacked = jnp.stack(parts)
    order = (me - jnp.arange(peers)) % peers
    return jnp.zeros_like(stacked).at[order].set(stacked)


ROW_PARTS = 4


def masked_apply_kernel(span_ref, env_ref, theta_ref, sec_j_ref, sec_i_ref, out_ref):
    step = pl.program_id(0)
    chain_w, rows_dev, depth = env_ref.shape
    rows_part = rows_dev // ROW_PARTS
    tile = span_ref[0] + step

    @pl.when(step == 0)
    def _():
        out_ref[...] = jnp.zeros_like(out_ref)

    for r in range(ROW_PARTS):
        rows = slice(r * rows_part, (r + 1) * rows_part)

        @pl.when((span_ref[2 * r] <= tile) & (tile <= span_ref[2 * r + 1]))
        def _():
            same = sec_i_ref[rows, :] == sec_j_ref[...]
            env = env_ref[:, rows, :]
            masked = jnp.where(same[None], env, jnp.zeros_like(env))
            masked = masked.reshape(chain_w * rows_part, depth)
            part = jnp.dot(masked, theta_ref[...], preferred_element_type=jnp.float32)
            out_ref[:, rows, :] += part.reshape(chain_w, rows_part, part.shape[1])


def masked_apply(env_loc, theta_all, sec_all, my_sec):
    chain_w, rows_dev, depth = env_loc.shape
    width = theta_all.shape[1]
    tiles = depth // K_TILE
    rows_part = rows_dev // ROW_PARTS
    bounds = []
    for r in range(ROW_PARTS):
        first = jnp.sum((sec_all < my_sec[r * rows_part]).astype(jnp.int32))
        last = jnp.sum((sec_all <= my_sec[(r + 1) * rows_part - 1]).astype(jnp.int32)) - 1
        bounds += [first // K_TILE, last // K_TILE]
    span = jnp.stack(bounds).astype(jnp.int32)

    def tile_of(step, span_ref):
        return jnp.minimum(span_ref[0] + step, span_ref[2 * ROW_PARTS - 1])

    grid_spec = pltpu.PrefetchScalarGridSpec(
        num_scalar_prefetch=1,
        grid=(tiles,),
        in_specs=[
            pl.BlockSpec((chain_w, rows_dev, K_TILE), lambda k, s: (0, 0, tile_of(k, s))),
            pl.BlockSpec((K_TILE, width), lambda k, s: (tile_of(k, s), 0)),
            pl.BlockSpec((1, K_TILE), lambda k, s: (0, tile_of(k, s))),
            pl.BlockSpec((rows_dev, 1), lambda k, s: (0, 0)),
        ],
        out_specs=pl.BlockSpec((chain_w, rows_dev, width), lambda k, s: (0, 0, 0)),
    )
    return pl.pallas_call(
        masked_apply_kernel,
        grid_spec=grid_spec,
        out_shape=jax.ShapeDtypeStruct((chain_w, rows_dev, width), jnp.float32),
        compiler_params=pltpu.CompilerParams(
            dimension_semantics=("arbitrary",), vmem_limit_bytes=48 * 1024 * 1024
        ),
    )(span, env_loc, theta_all, sec_all.reshape(1, depth), my_sec.reshape(rows_dev, 1))


def per_device(theta, left_env, sector_ids, local_ops, edge_env):
    rows_dev = theta.shape[1]
    width = theta.shape[2]
    chain_w = left_env.shape[1]
    phys = local_ops.shape[2]
    cols = width // phys
    theta_loc = theta[0]
    env_loc = left_env[0]
    sec_all = sector_ids[0]
    ops_loc = local_ops[0]
    my_block = lax.axis_index("blk")
    row_start = my_block * rows_dev
    my_sec = lax.dynamic_slice_in_dim(sec_all, row_start, rows_dev, 0)
    theta_all = lax.all_gather(theta_loc, "blk", axis=0, tiled=True)
    applied = masked_apply(env_loc, theta_all, sec_all, my_sec)
    applied = applied.reshape(chain_w, rows_dev, phys, cols)
    acted = jnp.einsum("wpq,wiqc->ipc", ops_loc, applied, precision=lax.Precision.HIGH)
    theta_f = theta_loc.astype(jnp.float32).reshape(rows_dev, phys, cols)
    partial_intersection = jnp.einsum(
        "ipc,ipd->cd", theta_f, acted, precision=lax.Precision.HIGH
    )
    intersection = butterfly_sum(partial_intersection, "blk")
    transfer = (
        intersection
        * jnp.sqrt(jnp.float32(cols))
        / jnp.sqrt(jnp.sum(intersection * intersection) + 1e-06)
    )
    transfers = gather_all(transfer, "sect")
    sect_no = lax.axis_index("sect")
    prefix = [edge_env]
    for step_no in range(lax.axis_size("sect")):
        prefix.append(matprod(prefix[-1], transfers[step_no]))
    prefix = jnp.stack(prefix)
    incoming = prefix[sect_no]
    outgoing = prefix[sect_no + 1]
    result = jnp.einsum("ipc,cd->ipd", acted, incoming, precision=lax.Precision.HIGH)
    updated = result.reshape(1, rows_dev, width).astype(jnp.bfloat16)
    return (updated, outgoing[None])


def solution(mesh):
    placed = (
        P("sect", "blk", None),
        P("sect", None, "blk", None),
        P("sect", None),
        P("sect", None, None, None),
        P(),
    )
    return jax.shard_map(
        per_device,
        mesh=mesh,
        in_specs=placed,
        out_specs=(P("sect", "blk", None), P("sect", None, None)),
        check_vma=False,
    )
```

```python
import functools

import jax
import jax.numpy as jnp
from jax import lax
from jax.experimental import pallas as pl
from jax.experimental.pallas import tpu as pltpu
from jax.sharding import PartitionSpec as P

K_TILE = 256


def matprod(first, second):
    return jnp.dot(first, second, precision=lax.Precision.HIGH)


def butterfly_sum(value, axis):
    peers = lax.axis_size(axis)
    step = 1
    while step < peers:
        pairs = [(i, i ^ step) for i in range(peers)]
        value = value + lax.ppermute(value, axis, pairs)
        step *= 2
    return value


def gather_all(value, axis):
    peers = lax.axis_size(axis)
    me = lax.axis_index(axis)
    parts = [value]
    for shift in range(1, peers):
        pairs = [(i, (i + shift) % peers) for i in range(peers)]
        parts.append(lax.ppermute(value, axis, pairs))
    stacked = jnp.stack(parts)
    order = (me - jnp.arange(peers)) % peers
    return jnp.zeros_like(stacked).at[order].set(stacked)


def masked_apply_kernel(span_ref, env_ref, theta_ref, sec_j_ref, sec_i_ref, out_ref):
    step = pl.program_id(0)

    @pl.when(step == 0)
    def _():
        out_ref[...] = jnp.zeros_like(out_ref)

    @pl.when(span_ref[0] + step <= span_ref[1])
    def _():
        same = sec_i_ref[...] == sec_j_ref[...]
        env = env_ref[...]
        masked = jnp.where(same[None], env, jnp.zeros_like(env))
        masked = masked.reshape(out_ref.shape[0], env.shape[2])
        out_ref[...] += jnp.dot(masked, theta_ref[...], preferred_element_type=jnp.float32)


def masked_apply(env_loc, theta_all, sec_all, my_sec):
    chain_w, rows_dev, depth = env_loc.shape
    width = theta_all.shape[1]
    tiles = depth // K_TILE
    first = jnp.sum((sec_all < my_sec[0]).astype(jnp.int32))
    last = jnp.sum((sec_all <= my_sec[-1]).astype(jnp.int32)) - 1
    span = jnp.stack([first // K_TILE, last // K_TILE]).astype(jnp.int32)

    def tile_of(step, span_ref):
        return jnp.minimum(span_ref[0] + step, span_ref[1])

    grid_spec = pltpu.PrefetchScalarGridSpec(
        num_scalar_prefetch=1,
        grid=(tiles,),
        in_specs=[
            pl.BlockSpec((chain_w, rows_dev, K_TILE), lambda k, s: (0, 0, tile_of(k, s))),
            pl.BlockSpec((K_TILE, width), lambda k, s: (tile_of(k, s), 0)),
            pl.BlockSpec((1, K_TILE), lambda k, s: (0, tile_of(k, s))),
            pl.BlockSpec((rows_dev, 1), lambda k, s: (0, 0)),
        ],
        out_specs=pl.BlockSpec((chain_w * rows_dev, width), lambda k, s: (0, 0)),
    )
    return pl.pallas_call(
        masked_apply_kernel,
        grid_spec=grid_spec,
        out_shape=jax.ShapeDtypeStruct((chain_w * rows_dev, width), jnp.float32),
        compiler_params=pltpu.CompilerParams(
            dimension_semantics=("arbitrary",), vmem_limit_bytes=48 * 1024 * 1024
        ),
    )(span, env_loc, theta_all, sec_all.reshape(1, depth), my_sec.reshape(rows_dev, 1))


def per_device(theta, left_env, sector_ids, local_ops, edge_env):
    rows_dev = theta.shape[1]
    width = theta.shape[2]
    chain_w = left_env.shape[1]
    phys = local_ops.shape[2]
    cols = width // phys
    theta_loc = theta[0]
    env_loc = left_env[0]
    sec_all = sector_ids[0]
    ops_loc = local_ops[0]
    my_block = lax.axis_index("blk")
    row_start = my_block * rows_dev
    my_sec = lax.dynamic_slice_in_dim(sec_all, row_start, rows_dev, 0)
    theta_all = lax.all_gather(theta_loc, "blk", axis=0, tiled=True)
    applied = masked_apply(env_loc, theta_all, sec_all, my_sec)
    applied = applied.reshape(chain_w, rows_dev, phys, cols)
    acted = jnp.einsum("wpq,wiqc->ipc", ops_loc, applied, precision=lax.Precision.HIGH)
    theta_f = theta_loc.astype(jnp.float32).reshape(rows_dev, phys, cols)
    partial_intersection = jnp.einsum(
        "ipc,ipd->cd", theta_f, acted, precision=lax.Precision.HIGH
    )
    intersection = butterfly_sum(partial_intersection, "blk")
    transfer = (
        intersection
        * jnp.sqrt(jnp.float32(cols))
        / jnp.sqrt(jnp.sum(intersection * intersection) + 1e-06)
    )
    transfers = gather_all(transfer, "sect")
    sect_no = lax.axis_index("sect")
    prefix = [edge_env]
    for step_no in range(lax.axis_size("sect")):
        prefix.append(matprod(prefix[-1], transfers[step_no]))
    prefix = jnp.stack(prefix)
    incoming = prefix[sect_no]
    outgoing = prefix[sect_no + 1]
    result = jnp.einsum("ipc,cd->ipd", acted, incoming, precision=lax.Precision.HIGH)
    updated = result.reshape(1, rows_dev, width).astype(jnp.bfloat16)
    return (updated, outgoing[None])


def solution(mesh):
    placed = (
        P("sect", "blk", None),
        P("sect", None, "blk", None),
        P("sect", None),
        P("sect", None, None, None),
        P(),
    )
    return jax.shard_map(
        per_device,
        mesh=mesh,
        in_specs=placed,
        out_specs=(P("sect", "blk", None), P("sect", None, None)),
        check_vma=False,
    )
```

```python
import functools

import jax
import jax.numpy as jnp
from jax import lax
from jax.experimental import pallas as pl
from jax.experimental.pallas import tpu as pltpu
from jax.sharding import PartitionSpec as P

K_TILE = 256


def matprod(first, second):
    return jnp.dot(first, second, precision=lax.Precision.HIGH)


def butterfly_sum(value, axis):
    peers = lax.axis_size(axis)
    step = 1
    while step < peers:
        pairs = [(i, i ^ step) for i in range(peers)]
        value = value + lax.ppermute(value, axis, pairs)
        step *= 2
    return value


def gather_all(value, axis):
    peers = lax.axis_size(axis)
    me = lax.axis_index(axis)
    parts = [value]
    for shift in range(1, peers):
        pairs = [(i, (i + shift) % peers) for i in range(peers)]
        parts.append(lax.ppermute(value, axis, pairs))
    stacked = jnp.stack(parts)
    order = (me - jnp.arange(peers)) % peers
    return jnp.zeros_like(stacked).at[order].set(stacked)


def masked_apply_kernel(span_ref, env_ref, theta_ref, sec_j_ref, sec_i_ref, out_ref):
    step = pl.program_id(0)

    @pl.when(step == 0)
    def _():
        out_ref[...] = jnp.zeros_like(out_ref)

    @pl.when(span_ref[0] + step <= span_ref[1])
    def _():
        same = sec_i_ref[...] == sec_j_ref[...]
        env = env_ref[...]
        masked = jnp.where(same[None], env, jnp.zeros_like(env))
        masked = masked.reshape(out_ref.shape[0], env.shape[2])
        out_ref[...] += jnp.dot(masked, theta_ref[...], preferred_element_type=jnp.float32)


def masked_apply(env_loc, theta_all, sec_all, my_sec):
    chain_w, rows_dev, depth = env_loc.shape
    width = theta_all.shape[1]
    tiles = depth // K_TILE
    first = jnp.sum((sec_all < my_sec[0]).astype(jnp.int32))
    last = jnp.sum((sec_all <= my_sec[-1]).astype(jnp.int32)) - 1
    span = jnp.stack([first // K_TILE, last // K_TILE]).astype(jnp.int32)

    def tile_of(step, span_ref):
        return jnp.minimum(span_ref[0] + step, span_ref[1])

    grid_spec = pltpu.PrefetchScalarGridSpec(
        num_scalar_prefetch=1,
        grid=(tiles,),
        in_specs=[
            pl.BlockSpec((chain_w, rows_dev, K_TILE), lambda k, s: (0, 0, tile_of(k, s))),
            pl.BlockSpec((K_TILE, width), lambda k, s: (tile_of(k, s), 0)),
            pl.BlockSpec((1, K_TILE), lambda k, s: (0, tile_of(k, s))),
            pl.BlockSpec((rows_dev, 1), lambda k, s: (0, 0)),
        ],
        out_specs=pl.BlockSpec((chain_w * rows_dev, width), lambda k, s: (0, 0)),
    )
    return pl.pallas_call(
        masked_apply_kernel,
        grid_spec=grid_spec,
        out_shape=jax.ShapeDtypeStruct((chain_w * rows_dev, width), jnp.float32),
        compiler_params=pltpu.CompilerParams(
            dimension_semantics=("arbitrary",), vmem_limit_bytes=48 * 1024 * 1024
        ),
    )(span, env_loc, theta_all, sec_all.reshape(1, depth), my_sec.reshape(rows_dev, 1))


def per_device(theta, left_env, sector_ids, local_ops, edge_env):
    rows_dev = theta.shape[1]
    width = theta.shape[2]
    chain_w = left_env.shape[1]
    phys = local_ops.shape[2]
    cols = width // phys
    theta_loc = theta[0]
    env_loc = left_env[0]
    sec_all = sector_ids[0]
    ops_loc = local_ops[0]
    my_block = lax.axis_index("blk")
    row_start = my_block * rows_dev
    my_sec = lax.dynamic_slice_in_dim(sec_all, row_start, rows_dev, 0)
    theta_all = lax.all_gather(theta_loc, "blk", axis=0, tiled=True)
    applied = masked_apply(env_loc, theta_all, sec_all, my_sec)
    applied = applied.reshape(chain_w, rows_dev, width)
    theta_f = theta_loc.astype(jnp.float32).reshape(rows_dev, phys, cols)
    theta_ops = jnp.einsum("wpq,ipc->qwic", ops_loc, theta_f, precision=lax.Precision.HIGHEST)
    partial_intersection = sum(
        jnp.einsum(
            "wic,wid->cd",
            theta_ops[q],
            applied[:, :, q * cols:(q + 1) * cols],
            precision=lax.Precision.HIGH,
        )
        for q in range(phys)
    )
    acted = jnp.einsum(
        "wpq,wiqc->ipc",
        ops_loc,
        applied.reshape(chain_w, rows_dev, phys, cols),
        precision=lax.Precision.HIGH,
    )
    intersection = butterfly_sum(partial_intersection, "blk")
    transfer = (
        intersection
        * jnp.sqrt(jnp.float32(cols))
        / jnp.sqrt(jnp.sum(intersection * intersection) + 1e-06)
    )
    transfers = gather_all(transfer, "sect")
    sect_no = lax.axis_index("sect")
    prefix = [edge_env]
    for step_no in range(lax.axis_size("sect")):
        prefix.append(matprod(prefix[-1], transfers[step_no]))
    prefix = jnp.stack(prefix)
    incoming = prefix[sect_no]
    outgoing = prefix[sect_no + 1]
    result = jnp.einsum("ipc,cd->ipd", acted, incoming, precision=lax.Precision.HIGH)
    updated = result.reshape(1, rows_dev, width).astype(jnp.bfloat16)
    return (updated, outgoing[None])


def solution(mesh):
    placed = (
        P("sect", "blk", None),
        P("sect", None, "blk", None),
        P("sect", None),
        P("sect", None, None, None),
        P(),
    )
    return jax.shard_map(
        per_device,
        mesh=mesh,
        in_specs=placed,
        out_specs=(P("sect", "blk", None), P("sect", None, None)),
        check_vma=False,
    )
```

```python
import functools

import jax
import jax.numpy as jnp
from jax import lax
from jax.experimental import pallas as pl
from jax.experimental.pallas import tpu as pltpu
from jax.sharding import PartitionSpec as P

K_TILE = 256


def matprod(first, second):
    return jnp.dot(first, second, precision=lax.Precision.HIGH)


def butterfly_sum(value, axis):
    peers = lax.axis_size(axis)
    step = 1
    while step < peers:
        pairs = [(i, i ^ step) for i in range(peers)]
        value = value + lax.ppermute(value, axis, pairs)
        step *= 2
    return value


def gather_all(value, axis):
    peers = lax.axis_size(axis)
    me = lax.axis_index(axis)
    parts = [value]
    for shift in range(1, peers):
        pairs = [(i, (i + shift) % peers) for i in range(peers)]
        parts.append(lax.ppermute(value, axis, pairs))
    stacked = jnp.stack(parts)
    order = (me - jnp.arange(peers)) % peers
    return jnp.zeros_like(stacked).at[order].set(stacked)


def masked_apply_kernel(span_ref, env_ref, theta_ref, sec_j_ref, sec_i_ref, out_ref):
    step = pl.program_id(0)

    @pl.when(step == 0)
    def _():
        out_ref[...] = jnp.zeros_like(out_ref)

    @pl.when(span_ref[0] + step <= span_ref[1])
    def _():
        env = env_ref[...]
        env = env.reshape(env.shape[0] * env.shape[1], env.shape[2])
        same = sec_i_ref[...] == sec_j_ref[...]
        masked = jnp.where(same, env, jnp.zeros_like(env))
        out_ref[...] += jnp.dot(masked, theta_ref[...], preferred_element_type=jnp.float32)


def masked_apply(env_loc, theta_all, sec_all, my_sec):
    chain_w, rows_dev, depth = env_loc.shape
    width = theta_all.shape[1]
    tiles = depth // K_TILE
    first = jnp.sum((sec_all < my_sec[0]).astype(jnp.int32))
    last = jnp.sum((sec_all <= my_sec[-1]).astype(jnp.int32)) - 1
    span = jnp.stack([first // K_TILE, last // K_TILE]).astype(jnp.int32)
    group = 16
    env_rows = jnp.transpose(env_loc, (1, 0, 2)).reshape(chain_w * rows_dev // group, group, depth)
    sec_rows = jnp.repeat(my_sec, chain_w).reshape(chain_w * rows_dev, 1)

    def tile_of(step, span_ref):
        return jnp.minimum(span_ref[0] + step, span_ref[1])

    grid_spec = pltpu.PrefetchScalarGridSpec(
        num_scalar_prefetch=1,
        grid=(tiles,),
        in_specs=[
            pl.BlockSpec((chain_w * rows_dev // group, group, K_TILE), lambda k, s: (0, 0, tile_of(k, s))),
            pl.BlockSpec((K_TILE, width), lambda k, s: (tile_of(k, s), 0)),
            pl.BlockSpec((1, K_TILE), lambda k, s: (0, tile_of(k, s))),
            pl.BlockSpec((chain_w * rows_dev, 1), lambda k, s: (0, 0)),
        ],
        out_specs=pl.BlockSpec((chain_w * rows_dev, width), lambda k, s: (0, 0)),
    )
    return pl.pallas_call(
        masked_apply_kernel,
        grid_spec=grid_spec,
        out_shape=jax.ShapeDtypeStruct((chain_w * rows_dev, width), jnp.float32),
        compiler_params=pltpu.CompilerParams(
            dimension_semantics=("arbitrary",), vmem_limit_bytes=48 * 1024 * 1024
        ),
    )(span, env_rows, theta_all, sec_all.reshape(1, depth), sec_rows)


def per_device(theta, left_env, sector_ids, local_ops, edge_env):
    rows_dev = theta.shape[1]
    width = theta.shape[2]
    chain_w = left_env.shape[1]
    phys = local_ops.shape[2]
    cols = width // phys
    theta_loc = theta[0]
    env_loc = left_env[0]
    sec_all = sector_ids[0]
    ops_loc = local_ops[0]
    my_block = lax.axis_index("blk")
    row_start = my_block * rows_dev
    my_sec = lax.dynamic_slice_in_dim(sec_all, row_start, rows_dev, 0)
    theta_all = lax.all_gather(theta_loc, "blk", axis=0, tiled=True)
    applied = masked_apply(env_loc, theta_all, sec_all, my_sec)
    applied = applied.reshape(rows_dev, chain_w, phys, cols)
    acted = jnp.einsum("wpq,iwqc->ipc", ops_loc, applied, precision=lax.Precision.HIGH)
    theta_f = theta_loc.astype(jnp.float32).reshape(rows_dev, phys, cols)
    partial_intersection = jnp.einsum(
        "ipc,ipd->cd", theta_f, acted, precision=lax.Precision.HIGH
    )
    intersection = butterfly_sum(partial_intersection, "blk")
    transfer = (
        intersection
        * jnp.sqrt(jnp.float32(cols))
        / jnp.sqrt(jnp.sum(intersection * intersection) + 1e-06)
    )
    transfers = gather_all(transfer, "sect")
    sect_no = lax.axis_index("sect")
    prefix = [edge_env]
    for step_no in range(lax.axis_size("sect")):
        prefix.append(matprod(prefix[-1], transfers[step_no]))
    prefix = jnp.stack(prefix)
    incoming = prefix[sect_no]
    outgoing = prefix[sect_no + 1]
    result = jnp.einsum("ipc,cd->ipd", acted, incoming, precision=lax.Precision.HIGH)
    updated = result.reshape(1, rows_dev, width).astype(jnp.bfloat16)
    return (updated, outgoing[None])


def solution(mesh):
    placed = (
        P("sect", "blk", None),
        P("sect", None, "blk", None),
        P("sect", None),
        P("sect", None, None, None),
        P(),
    )
    return jax.shard_map(
        per_device,
        mesh=mesh,
        in_specs=placed,
        out_specs=(P("sect", "blk", None), P("sect", None, None)),
        check_vma=False,
    )
```

```python
import functools

import jax
import jax.numpy as jnp
from jax import lax
from jax.experimental import pallas as pl
from jax.experimental.pallas import tpu as pltpu
from jax.sharding import PartitionSpec as P

K_TILE = 256


def matprod(first, second):
    return jnp.dot(first, second, precision=lax.Precision.HIGH)


def butterfly_sum(value, axis):
    peers = lax.axis_size(axis)
    step = 1
    while step < peers:
        pairs = [(i, i ^ step) for i in range(peers)]
        value = value + lax.ppermute(value, axis, pairs)
        step *= 2
    return value


def gather_all(value, axis):
    peers = lax.axis_size(axis)
    me = lax.axis_index(axis)
    parts = [value]
    for shift in range(1, peers):
        pairs = [(i, (i + shift) % peers) for i in range(peers)]
        parts.append(lax.ppermute(value, axis, pairs))
    stacked = jnp.stack(parts)
    order = (me - jnp.arange(peers)) % peers
    return jnp.zeros_like(stacked).at[order].set(stacked)


def masked_apply_kernel(span_ref, env_ref, theta_ref, sec_j_ref, sec_i_ref, out_ref):
    step = pl.program_id(0)

    def product():
        env = env_ref[...]
        env = env.reshape(env.shape[0] * env.shape[1], env.shape[2])
        same = sec_i_ref[...] == sec_j_ref[...]
        masked = jnp.where(same, env, jnp.zeros_like(env))
        return jnp.dot(masked, theta_ref[...], preferred_element_type=jnp.float32)

    @pl.when(step == 0)
    def _():
        out_ref[...] = product()

    @pl.when((step > 0) & (span_ref[0] + step <= span_ref[1]))
    def _():
        out_ref[...] += product()


def masked_apply(env_loc, theta_all, sec_all, my_sec):
    chain_w, rows_dev, depth = env_loc.shape
    width = theta_all.shape[1]
    tiles = depth // K_TILE
    first = jnp.sum((sec_all < my_sec[0]).astype(jnp.int32))
    last = jnp.sum((sec_all <= my_sec[-1]).astype(jnp.int32)) - 1
    span = jnp.stack([first // K_TILE, last // K_TILE]).astype(jnp.int32)
    group = 16
    env_rows = jnp.transpose(env_loc, (1, 0, 2)).reshape(chain_w * rows_dev // group, group, depth)
    sec_rows = jnp.repeat(my_sec, chain_w).reshape(chain_w * rows_dev, 1)

    def tile_of(step, span_ref):
        return jnp.minimum(span_ref[0] + step, span_ref[1])

    grid_spec = pltpu.PrefetchScalarGridSpec(
        num_scalar_prefetch=1,
        grid=(tiles,),
        in_specs=[
            pl.BlockSpec((chain_w * rows_dev // group, group, K_TILE), lambda k, s: (0, 0, tile_of(k, s))),
            pl.BlockSpec((K_TILE, width), lambda k, s: (tile_of(k, s), 0)),
            pl.BlockSpec((1, K_TILE), lambda k, s: (0, tile_of(k, s))),
            pl.BlockSpec((chain_w * rows_dev, 1), lambda k, s: (0, 0)),
        ],
        out_specs=pl.BlockSpec((chain_w * rows_dev, width), lambda k, s: (0, 0)),
    )
    return pl.pallas_call(
        masked_apply_kernel,
        grid_spec=grid_spec,
        out_shape=jax.ShapeDtypeStruct((chain_w * rows_dev, width), jnp.float32),
        compiler_params=pltpu.CompilerParams(
            dimension_semantics=("arbitrary",), vmem_limit_bytes=48 * 1024 * 1024
        ),
    )(span, env_rows, theta_all, sec_all.reshape(1, depth), sec_rows)


def per_device(theta, left_env, sector_ids, local_ops, edge_env):
    rows_dev = theta.shape[1]
    width = theta.shape[2]
    chain_w = left_env.shape[1]
    phys = local_ops.shape[2]
    cols = width // phys
    theta_loc = theta[0]
    env_loc = left_env[0]
    sec_all = sector_ids[0]
    ops_loc = local_ops[0]
    my_block = lax.axis_index("blk")
    row_start = my_block * rows_dev
    my_sec = lax.dynamic_slice_in_dim(sec_all, row_start, rows_dev, 0)
    theta_all = lax.all_gather(theta_loc, "blk", axis=0, tiled=True)
    applied = masked_apply(env_loc, theta_all, sec_all, my_sec)
    applied = applied.reshape(rows_dev, chain_w, phys, cols)
    acted = jnp.einsum("wpq,iwqc->ipc", ops_loc, applied, precision=lax.Precision.HIGH)
    theta_f = theta_loc.astype(jnp.float32).reshape(rows_dev, phys, cols)
    partial_intersection = jnp.einsum(
        "ipc,ipd->cd", theta_f, acted, precision=lax.Precision.HIGH
    )
    intersection = butterfly_sum(partial_intersection, "blk")
    transfer = (
        intersection
        * jnp.sqrt(jnp.float32(cols))
        / jnp.sqrt(jnp.sum(intersection * intersection) + 1e-06)
    )
    transfers = gather_all(transfer, "sect")
    sect_no = lax.axis_index("sect")
    prefix = [edge_env]
    for step_no in range(lax.axis_size("sect")):
        prefix.append(matprod(prefix[-1], transfers[step_no]))
    prefix = jnp.stack(prefix)
    incoming = prefix[sect_no]
    outgoing = prefix[sect_no + 1]
    result = jnp.einsum("ipc,cd->ipd", acted, incoming, precision=lax.Precision.HIGH)
    updated = result.reshape(1, rows_dev, width).astype(jnp.bfloat16)
    return (updated, outgoing[None])


def solution(mesh):
    placed = (
        P("sect", "blk", None),
        P("sect", None, "blk", None),
        P("sect", None),
        P("sect", None, None, None),
        P(),
    )
    return jax.shard_map(
        per_device,
        mesh=mesh,
        in_specs=placed,
        out_specs=(P("sect", "blk", None), P("sect", None, None)),
        check_vma=False,
    )
```

```python
import functools

import jax
import jax.numpy as jnp
from jax import lax
from jax.experimental import pallas as pl
from jax.experimental.pallas import tpu as pltpu
from jax.sharding import PartitionSpec as P

K_TILE = 256


def matprod(first, second):
    return jnp.dot(first, second, precision=lax.Precision.HIGH)


def grouped_sum(value, axis, sizes):
    peers = lax.axis_size(axis)
    stride = 1
    for size in sizes:
        total = value
        for shift in range(1, size):
            pairs = []
            for i in range(peers):
                digit = (i // stride) % size
                pairs.append((i, i + ((digit + shift) % size - digit) * stride))
            total = total + lax.ppermute(value, axis, pairs)
        value = total
        stride *= size
    return value


def gather_all(value, axis):
    peers = lax.axis_size(axis)
    me = lax.axis_index(axis)
    parts = [value]
    for shift in range(1, peers):
        pairs = [(i, (i + shift) % peers) for i in range(peers)]
        parts.append(lax.ppermute(value, axis, pairs))
    stacked = jnp.stack(parts)
    order = (me - jnp.arange(peers)) % peers
    return jnp.zeros_like(stacked).at[order].set(stacked)


def masked_apply_kernel(span_ref, env_ref, theta_ref, sec_j_ref, sec_i_ref, out_ref):
    step = pl.program_id(0)

    def product():
        env = env_ref[...]
        env = env.reshape(env.shape[0] * env.shape[1], env.shape[2])
        same = sec_i_ref[...] == sec_j_ref[...]
        masked = jnp.where(same, env, jnp.zeros_like(env))
        return jnp.dot(masked, theta_ref[...], preferred_element_type=jnp.float32)

    @pl.when(step == 0)
    def _():
        out_ref[...] = product()

    @pl.when((step > 0) & (span_ref[0] + step <= span_ref[1]))
    def _():
        out_ref[...] += product()


def masked_apply(env_loc, theta_all, sec_all, my_sec):
    chain_w, rows_dev, depth = env_loc.shape
    width = theta_all.shape[1]
    tiles = depth // K_TILE
    first = jnp.sum((sec_all < my_sec[0]).astype(jnp.int32))
    last = jnp.sum((sec_all <= my_sec[-1]).astype(jnp.int32)) - 1
    span = jnp.stack([first // K_TILE, last // K_TILE]).astype(jnp.int32)
    group = 16
    env_rows = jnp.transpose(env_loc, (1, 0, 2)).reshape(chain_w * rows_dev // group, group, depth)
    sec_rows = jnp.repeat(my_sec, chain_w).reshape(chain_w * rows_dev, 1)

    def tile_of(step, span_ref):
        return jnp.minimum(span_ref[0] + step, span_ref[1])

    grid_spec = pltpu.PrefetchScalarGridSpec(
        num_scalar_prefetch=1,
        grid=(tiles,),
        in_specs=[
            pl.BlockSpec((chain_w * rows_dev // group, group, K_TILE), lambda k, s: (0, 0, tile_of(k, s))),
            pl.BlockSpec((K_TILE, width), lambda k, s: (tile_of(k, s), 0)),
            pl.BlockSpec((1, K_TILE), lambda k, s: (0, tile_of(k, s))),
            pl.BlockSpec((chain_w * rows_dev, 1), lambda k, s: (0, 0)),
        ],
        out_specs=pl.BlockSpec((chain_w * rows_dev, width), lambda k, s: (0, 0)),
    )
    return pl.pallas_call(
        masked_apply_kernel,
        grid_spec=grid_spec,
        out_shape=jax.ShapeDtypeStruct((chain_w * rows_dev, width), jnp.float32),
        compiler_params=pltpu.CompilerParams(
            dimension_semantics=("arbitrary",), vmem_limit_bytes=48 * 1024 * 1024
        ),
    )(span, env_rows, theta_all, sec_all.reshape(1, depth), sec_rows)


def per_device(theta, left_env, sector_ids, local_ops, edge_env):
    rows_dev = theta.shape[1]
    width = theta.shape[2]
    chain_w = left_env.shape[1]
    phys = local_ops.shape[2]
    cols = width // phys
    theta_loc = theta[0]
    env_loc = left_env[0]
    sec_all = sector_ids[0]
    ops_loc = local_ops[0]
    my_block = lax.axis_index("blk")
    row_start = my_block * rows_dev
    my_sec = lax.dynamic_slice_in_dim(sec_all, row_start, rows_dev, 0)
    theta_all = lax.all_gather(theta_loc, "blk", axis=0, tiled=True)
    applied = masked_apply(env_loc, theta_all, sec_all, my_sec)
    applied = applied.reshape(rows_dev, chain_w, phys, cols)
    acted = jnp.einsum("wpq,iwqc->ipc", ops_loc, applied, precision=lax.Precision.HIGH)
    theta_f = theta_loc.astype(jnp.float32).reshape(rows_dev, phys, cols)
    partial_intersection = jnp.einsum(
        "ipc,ipd->cd", theta_f, acted, precision=lax.Precision.HIGH
    )
    blk_peers = lax.axis_size("blk")
    intersection = grouped_sum(partial_intersection, "blk", (2, 4, blk_peers // 8))
    transfer = (
        intersection
        * jnp.sqrt(jnp.float32(cols))
        / jnp.sqrt(jnp.sum(intersection * intersection) + 1e-06)
    )
    transfers = gather_all(transfer, "sect")
    sect_no = lax.axis_index("sect")
    prefix = [edge_env]
    for step_no in range(lax.axis_size("sect")):
        prefix.append(matprod(prefix[-1], transfers[step_no]))
    prefix = jnp.stack(prefix)
    incoming = prefix[sect_no]
    outgoing = prefix[sect_no + 1]
    result = jnp.einsum("ipc,cd->ipd", acted, incoming, precision=lax.Precision.HIGH)
    updated = result.reshape(1, rows_dev, width).astype(jnp.bfloat16)
    return (updated, outgoing[None])


def solution(mesh):
    placed = (
        P("sect", "blk", None),
        P("sect", None, "blk", None),
        P("sect", None),
        P("sect", None, None, None),
        P(),
    )
    return jax.shard_map(
        per_device,
        mesh=mesh,
        in_specs=placed,
        out_specs=(P("sect", "blk", None), P("sect", None, None)),
        check_vma=False,
    )
```

```python
import functools

import jax
import jax.numpy as jnp
from jax import lax
from jax.experimental import pallas as pl
from jax.experimental.pallas import tpu as pltpu
from jax.sharding import PartitionSpec as P

K_TILE = 256


def matprod(first, second):
    return jnp.dot(first, second, precision=lax.Precision.HIGH)


def grouped_sum(value, axis, sizes):
    peers = lax.axis_size(axis)
    stride = 1
    for size in sizes:
        total = value
        for shift in range(1, size):
            pairs = []
            for i in range(peers):
                digit = (i // stride) % size
                pairs.append((i, i + ((digit + shift) % size - digit) * stride))
            total = total + lax.ppermute(value, axis, pairs)
        value = total
        stride *= size
    return value


def gather_all(value, axis):
    peers = lax.axis_size(axis)
    me = lax.axis_index(axis)
    parts = [value]
    for shift in range(1, peers):
        pairs = [(i, (i + shift) % peers) for i in range(peers)]
        parts.append(lax.ppermute(value, axis, pairs))
    stacked = jnp.stack(parts)
    order = (me - jnp.arange(peers)) % peers
    return jnp.zeros_like(stacked).at[order].set(stacked)


def masked_apply_kernel(span_ref, env_ref, theta_ref, sec_j_ref, sec_i_ref, out_ref):
    step = pl.program_id(0)

    def product():
        env = env_ref[...]
        env = env.reshape(env.shape[0] * env.shape[1], env.shape[2])
        same = sec_i_ref[...] == sec_j_ref[...]
        masked = jnp.where(same, env, jnp.zeros_like(env))
        return jnp.dot(masked, theta_ref[...], preferred_element_type=jnp.float32)

    @pl.when(step == 0)
    def _():
        out_ref[...] = product()

    @pl.when((step > 0) & (span_ref[0] + step <= span_ref[1]))
    def _():
        out_ref[...] += product()


def masked_apply(env_loc, theta_all, sec_all, my_sec):
    chain_w, rows_dev, depth = env_loc.shape
    width = theta_all.shape[1]
    tiles = depth // K_TILE
    first = jnp.sum((sec_all < my_sec[0]).astype(jnp.int32))
    last = jnp.sum((sec_all <= my_sec[-1]).astype(jnp.int32)) - 1
    span = jnp.stack([first // K_TILE, last // K_TILE]).astype(jnp.int32)
    group = 16
    env_rows = jnp.transpose(env_loc, (1, 0, 2)).reshape(chain_w * rows_dev // group, group, depth)
    sec_rows = jnp.repeat(my_sec, chain_w).reshape(chain_w * rows_dev, 1)

    def tile_of(step, span_ref):
        return jnp.minimum(span_ref[0] + step, span_ref[1])

    grid_spec = pltpu.PrefetchScalarGridSpec(
        num_scalar_prefetch=1,
        grid=(tiles,),
        in_specs=[
            pl.BlockSpec((chain_w * rows_dev // group, group, K_TILE), lambda k, s: (0, 0, tile_of(k, s))),
            pl.BlockSpec((K_TILE, width), lambda k, s: (tile_of(k, s), 0)),
            pl.BlockSpec((1, K_TILE), lambda k, s: (0, tile_of(k, s))),
            pl.BlockSpec((chain_w * rows_dev, 1), lambda k, s: (0, 0)),
        ],
        out_specs=pl.BlockSpec((chain_w * rows_dev, width), lambda k, s: (0, 0)),
    )
    return pl.pallas_call(
        masked_apply_kernel,
        grid_spec=grid_spec,
        out_shape=jax.ShapeDtypeStruct((chain_w * rows_dev, width), jnp.float32),
        compiler_params=pltpu.CompilerParams(
            dimension_semantics=("arbitrary",), vmem_limit_bytes=48 * 1024 * 1024
        ),
    )(span, env_rows, theta_all, sec_all.reshape(1, depth), sec_rows)


def per_device(theta, left_env, sector_ids, local_ops, edge_env):
    rows_dev = theta.shape[1]
    width = theta.shape[2]
    chain_w = left_env.shape[1]
    phys = local_ops.shape[2]
    cols = width // phys
    theta_loc = theta[0]
    env_loc = left_env[0]
    sec_all = sector_ids[0]
    ops_loc = local_ops[0]
    my_block = lax.axis_index("blk")
    row_start = my_block * rows_dev
    my_sec = lax.dynamic_slice_in_dim(sec_all, row_start, rows_dev, 0)
    theta_all = lax.all_gather(theta_loc, "blk", axis=0, tiled=True)
    applied = masked_apply(env_loc, theta_all, sec_all, my_sec)
    applied = applied.reshape(rows_dev, chain_w, phys, cols)
    acted = jnp.einsum("wpq,iwqc->ipc", ops_loc, applied, precision=lax.Precision.HIGH)
    theta_f = theta_loc.astype(jnp.float32).reshape(rows_dev, phys, cols)
    partial_intersection = jnp.einsum(
        "ipc,ipd->cd", theta_f, acted, precision=lax.Precision.HIGH
    )
    blk_peers = lax.axis_size("blk")
    intersection = grouped_sum(partial_intersection, "blk", (8, blk_peers // 8))
    transfer = (
        intersection
        * jnp.sqrt(jnp.float32(cols))
        / jnp.sqrt(jnp.sum(intersection * intersection) + 1e-06)
    )
    transfers = gather_all(transfer, "sect")
    sect_no = lax.axis_index("sect")
    prefix = [edge_env]
    for step_no in range(lax.axis_size("sect")):
        prefix.append(matprod(prefix[-1], transfers[step_no]))
    prefix = jnp.stack(prefix)
    incoming = prefix[sect_no]
    outgoing = prefix[sect_no + 1]
    result = jnp.einsum("ipc,cd->ipd", acted, incoming, precision=lax.Precision.HIGH)
    updated = result.reshape(1, rows_dev, width).astype(jnp.bfloat16)
    return (updated, outgoing[None])


def solution(mesh):
    placed = (
        P("sect", "blk", None),
        P("sect", None, "blk", None),
        P("sect", None),
        P("sect", None, None, None),
        P(),
    )
    return jax.shard_map(
        per_device,
        mesh=mesh,
        in_specs=placed,
        out_specs=(P("sect", "blk", None), P("sect", None, None)),
        check_vma=False,
    )
```

```python
import functools

import jax
import jax.numpy as jnp
from jax import lax
from jax.experimental import pallas as pl
from jax.experimental.pallas import tpu as pltpu
from jax.sharding import PartitionSpec as P

K_TILE = 256


def matprod(first, second):
    return jnp.dot(first, second, precision=lax.Precision.HIGH)


def grouped_sum(value, axis, sizes):
    peers = lax.axis_size(axis)
    stride = 1
    for size in sizes:
        total = value
        for shift in range(1, size):
            pairs = []
            for i in range(peers):
                digit = (i // stride) % size
                pairs.append((i, i + ((digit + shift) % size - digit) * stride))
            total = total + lax.ppermute(value, axis, pairs)
        value = total
        stride *= size
    return value


def gather_all(value, axis):
    peers = lax.axis_size(axis)
    me = lax.axis_index(axis)
    parts = [value]
    for shift in range(1, peers):
        pairs = [(i, i + shift) for i in range(peers - shift)]
        parts.append(lax.ppermute(value, axis, pairs))
    stacked = jnp.stack(parts)
    order = (me - jnp.arange(peers)) % peers
    return jnp.zeros_like(stacked).at[order].set(stacked)


def masked_apply_kernel(span_ref, env_ref, theta_ref, sec_j_ref, sec_i_ref, out_ref):
    step = pl.program_id(0)

    def product():
        env = env_ref[...]
        env = env.reshape(env.shape[0] * env.shape[1], env.shape[2])
        same = sec_i_ref[...] == sec_j_ref[...]
        masked = jnp.where(same, env, jnp.zeros_like(env))
        return jnp.dot(masked, theta_ref[...], preferred_element_type=jnp.float32)

    @pl.when(step == 0)
    def _():
        out_ref[...] = product()

    @pl.when((step > 0) & (span_ref[0] + step <= span_ref[1]))
    def _():
        out_ref[...] += product()


def masked_apply(env_loc, theta_all, sec_all, my_sec):
    chain_w, rows_dev, depth = env_loc.shape
    width = theta_all.shape[1]
    tiles = depth // K_TILE
    first = jnp.sum((sec_all < my_sec[0]).astype(jnp.int32))
    last = jnp.sum((sec_all <= my_sec[-1]).astype(jnp.int32)) - 1
    span = jnp.stack([first // K_TILE, last // K_TILE]).astype(jnp.int32)
    group = 16
    env_rows = jnp.transpose(env_loc, (1, 0, 2)).reshape(chain_w * rows_dev // group, group, depth)
    sec_rows = jnp.repeat(my_sec, chain_w).reshape(chain_w * rows_dev, 1)

    def tile_of(step, span_ref):
        return jnp.minimum(span_ref[0] + step, span_ref[1])

    grid_spec = pltpu.PrefetchScalarGridSpec(
        num_scalar_prefetch=1,
        grid=(tiles,),
        in_specs=[
            pl.BlockSpec((chain_w * rows_dev // group, group, K_TILE), lambda k, s: (0, 0, tile_of(k, s))),
            pl.BlockSpec((K_TILE, width), lambda k, s: (tile_of(k, s), 0)),
            pl.BlockSpec((1, K_TILE), lambda k, s: (0, tile_of(k, s))),
            pl.BlockSpec((chain_w * rows_dev, 1), lambda k, s: (0, 0)),
        ],
        out_specs=pl.BlockSpec((chain_w * rows_dev, width), lambda k, s: (0, 0)),
    )
    return pl.pallas_call(
        masked_apply_kernel,
        grid_spec=grid_spec,
        out_shape=jax.ShapeDtypeStruct((chain_w * rows_dev, width), jnp.float32),
        compiler_params=pltpu.CompilerParams(
            dimension_semantics=("arbitrary",), vmem_limit_bytes=48 * 1024 * 1024
        ),
    )(span, env_rows, theta_all, sec_all.reshape(1, depth), sec_rows)


def per_device(theta, left_env, sector_ids, local_ops, edge_env):
    rows_dev = theta.shape[1]
    width = theta.shape[2]
    chain_w = left_env.shape[1]
    phys = local_ops.shape[2]
    cols = width // phys
    theta_loc = theta[0]
    env_loc = left_env[0]
    sec_all = sector_ids[0]
    ops_loc = local_ops[0]
    my_block = lax.axis_index("blk")
    row_start = my_block * rows_dev
    my_sec = lax.dynamic_slice_in_dim(sec_all, row_start, rows_dev, 0)
    theta_all = lax.all_gather(theta_loc, "blk", axis=0, tiled=True)
    applied = masked_apply(env_loc, theta_all, sec_all, my_sec)
    applied = applied.reshape(rows_dev, chain_w, phys, cols)
    acted = jnp.einsum("wpq,iwqc->ipc", ops_loc, applied, precision=lax.Precision.HIGH)
    theta_f = theta_loc.astype(jnp.float32).reshape(rows_dev, phys, cols)
    partial_intersection = jnp.einsum(
        "ipc,ipd->cd", theta_f, acted, precision=lax.Precision.HIGH
    )
    blk_peers = lax.axis_size("blk")
    intersection = grouped_sum(partial_intersection, "blk", (2, 4, blk_peers // 8))
    transfer = (
        intersection
        * jnp.sqrt(jnp.float32(cols))
        / jnp.sqrt(jnp.sum(intersection * intersection) + 1e-06)
    )
    transfers = gather_all(transfer, "sect")
    sect_no = lax.axis_index("sect")
    prefix = [edge_env]
    for step_no in range(lax.axis_size("sect")):
        prefix.append(matprod(prefix[-1], transfers[step_no]))
    prefix = jnp.stack(prefix)
    incoming = prefix[sect_no]
    outgoing = prefix[sect_no + 1]
    result = jnp.einsum("ipc,cd->ipd", acted, incoming, precision=lax.Precision.HIGH)
    updated = result.reshape(1, rows_dev, width).astype(jnp.bfloat16)
    return (updated, outgoing[None])


def solution(mesh):
    placed = (
        P("sect", "blk", None),
        P("sect", None, "blk", None),
        P("sect", None),
        P("sect", None, None, None),
        P(),
    )
    return jax.shard_map(
        per_device,
        mesh=mesh,
        in_specs=placed,
        out_specs=(P("sect", "blk", None), P("sect", None, None)),
        check_vma=False,
    )
```

```python
import functools

import jax
import jax.numpy as jnp
from jax import lax
from jax.experimental import pallas as pl
from jax.experimental.pallas import tpu as pltpu
from jax.sharding import PartitionSpec as P

K_TILE = 256


def matprod(first, second):
    return jnp.dot(first, second, precision=lax.Precision.HIGH)


def grouped_sum(value, axis, sizes):
    peers = lax.axis_size(axis)
    stride = 1
    for size in sizes:
        total = value
        for shift in range(1, size):
            pairs = []
            for i in range(peers):
                digit = (i // stride) % size
                pairs.append((i, i + ((digit + shift) % size - digit) * stride))
            total = total + lax.ppermute(value, axis, pairs)
        value = total
        stride *= size
    return value


def gather_all(value, axis):
    peers = lax.axis_size(axis)
    me = lax.axis_index(axis)
    parts = [value]
    for shift in range(1, peers):
        pairs = [(i, (i + shift) % peers) for i in range(peers)]
        parts.append(lax.ppermute(value, axis, pairs))
    stacked = jnp.stack(parts)
    order = (me - jnp.arange(peers)) % peers
    return jnp.zeros_like(stacked).at[order].set(stacked)


def masked_apply_kernel(span_ref, env_ref, theta_ref, out_ref):
    step = pl.program_id(0)

    def product():
        env = env_ref[...]
        env = env.reshape(env.shape[0] * env.shape[1], env.shape[2])
        return jnp.dot(env, theta_ref[...], preferred_element_type=jnp.float32)

    @pl.when(step == 0)
    def _():
        out_ref[...] = product()

    @pl.when((step > 0) & (span_ref[0] + step <= span_ref[1]))
    def _():
        out_ref[...] += product()


def masked_apply(env_loc, theta_all, sec_all, my_sec):
    chain_w, rows_dev, depth = env_loc.shape
    width = theta_all.shape[1]
    tiles = depth // K_TILE
    first = jnp.sum((sec_all < my_sec[0]).astype(jnp.int32))
    last = jnp.sum((sec_all <= my_sec[-1]).astype(jnp.int32)) - 1
    span = jnp.stack([first // K_TILE, last // K_TILE]).astype(jnp.int32)
    group = 16
    same = my_sec[:, None] == sec_all[None, :]
    masked = jnp.where(same[None], env_loc, jnp.zeros_like(env_loc))
    env_rows = jnp.transpose(masked, (1, 0, 2)).reshape(chain_w * rows_dev // group, group, depth)

    def tile_of(step, span_ref):
        return jnp.minimum(span_ref[0] + step, span_ref[1])

    grid_spec = pltpu.PrefetchScalarGridSpec(
        num_scalar_prefetch=1,
        grid=(tiles,),
        in_specs=[
            pl.BlockSpec((chain_w * rows_dev // group, group, K_TILE), lambda k, s: (0, 0, tile_of(k, s))),
            pl.BlockSpec((K_TILE, width), lambda k, s: (tile_of(k, s), 0)),
        ],
        out_specs=pl.BlockSpec((chain_w * rows_dev, width), lambda k, s: (0, 0)),
    )
    return pl.pallas_call(
        masked_apply_kernel,
        grid_spec=grid_spec,
        out_shape=jax.ShapeDtypeStruct((chain_w * rows_dev, width), jnp.float32),
        compiler_params=pltpu.CompilerParams(
            dimension_semantics=("arbitrary",), vmem_limit_bytes=48 * 1024 * 1024
        ),
    )(span, env_rows, theta_all)


def per_device(theta, left_env, sector_ids, local_ops, edge_env):
    rows_dev = theta.shape[1]
    width = theta.shape[2]
    chain_w = left_env.shape[1]
    phys = local_ops.shape[2]
    cols = width // phys
    theta_loc = theta[0]
    env_loc = left_env[0]
    sec_all = sector_ids[0]
    ops_loc = local_ops[0]
    my_block = lax.axis_index("blk")
    row_start = my_block * rows_dev
    my_sec = lax.dynamic_slice_in_dim(sec_all, row_start, rows_dev, 0)
    theta_all = lax.all_gather(theta_loc, "blk", axis=0, tiled=True)
    applied = masked_apply(env_loc, theta_all, sec_all, my_sec)
    applied = applied.reshape(rows_dev, chain_w, phys, cols)
    acted = jnp.einsum("wpq,iwqc->ipc", ops_loc, applied, precision=lax.Precision.HIGH)
    theta_f = theta_loc.astype(jnp.float32).reshape(rows_dev, phys, cols)
    partial_intersection = jnp.einsum(
        "ipc,ipd->cd", theta_f, acted, precision=lax.Precision.HIGH
    )
    blk_peers = lax.axis_size("blk")
    intersection = grouped_sum(partial_intersection, "blk", (2, 4, blk_peers // 8))
    transfer = (
        intersection
        * jnp.sqrt(jnp.float32(cols))
        / jnp.sqrt(jnp.sum(intersection * intersection) + 1e-06)
    )
    transfers = gather_all(transfer, "sect")
    sect_no = lax.axis_index("sect")
    prefix = [edge_env]
    for step_no in range(lax.axis_size("sect")):
        prefix.append(matprod(prefix[-1], transfers[step_no]))
    prefix = jnp.stack(prefix)
    incoming = prefix[sect_no]
    outgoing = prefix[sect_no + 1]
    result = jnp.einsum("ipc,cd->ipd", acted, incoming, precision=lax.Precision.HIGH)
    updated = result.reshape(1, rows_dev, width).astype(jnp.bfloat16)
    return (updated, outgoing[None])


def solution(mesh):
    placed = (
        P("sect", "blk", None),
        P("sect", None, "blk", None),
        P("sect", None),
        P("sect", None, None, None),
        P(),
    )
    return jax.shard_map(
        per_device,
        mesh=mesh,
        in_specs=placed,
        out_specs=(P("sect", "blk", None), P("sect", None, None)),
        check_vma=False,
    )
```

```python
import functools

import jax
import jax.numpy as jnp
from jax import lax
from jax.experimental import pallas as pl
from jax.experimental.pallas import tpu as pltpu
from jax.sharding import PartitionSpec as P

K_TILE = 256


def matprod(first, second):
    return jnp.dot(first, second, precision=lax.Precision.HIGH)


def grouped_sum(value, axis, sizes):
    peers = lax.axis_size(axis)
    stride = 1
    for size in sizes:
        total = value
        for shift in range(1, size):
            pairs = []
            for i in range(peers):
                digit = (i // stride) % size
                pairs.append((i, i + ((digit + shift) % size - digit) * stride))
            total = total + lax.ppermute(value, axis, pairs)
        value = total
        stride *= size
    return value


def gather_all(value, axis):
    peers = lax.axis_size(axis)
    parts = [value]
    for shift in range(1, peers):
        pairs = [(i, (i + shift) % peers) for i in range(peers)]
        parts.append(lax.ppermute(value, axis, pairs))
    return jnp.stack(parts)


def masked_apply_kernel(span_ref, env_ref, theta_ref, sec_j_ref, sec_i_ref, out_ref):
    step = pl.program_id(0)

    def product():
        env = env_ref[...]
        env = env.reshape(env.shape[0] * env.shape[1], env.shape[2])
        same = sec_i_ref[...] == sec_j_ref[...]
        masked = jnp.where(same, env, jnp.zeros_like(env))
        return jnp.dot(masked, theta_ref[...], preferred_element_type=jnp.float32)

    @pl.when(step == 0)
    def _():
        out_ref[...] = product()

    @pl.when((step > 0) & (span_ref[0] + step <= span_ref[1]))
    def _():
        out_ref[...] += product()


def masked_apply(env_loc, theta_all, sec_all, my_sec):
    chain_w, rows_dev, depth = env_loc.shape
    width = theta_all.shape[1]
    tiles = depth // K_TILE
    first = jnp.sum((sec_all < my_sec[0]).astype(jnp.int32))
    last = jnp.sum((sec_all <= my_sec[-1]).astype(jnp.int32)) - 1
    span = jnp.stack([first // K_TILE, last // K_TILE]).astype(jnp.int32)
    group = 16
    env_rows = jnp.transpose(env_loc, (1, 0, 2)).reshape(chain_w * rows_dev // group, group, depth)
    sec_rows = jnp.repeat(my_sec, chain_w).reshape(chain_w * rows_dev, 1)

    def tile_of(step, span_ref):
        return jnp.minimum(span_ref[0] + step, span_ref[1])

    grid_spec = pltpu.PrefetchScalarGridSpec(
        num_scalar_prefetch=1,
        grid=(tiles,),
        in_specs=[
            pl.BlockSpec((chain_w * rows_dev // group, group, K_TILE), lambda k, s: (0, 0, tile_of(k, s))),
            pl.BlockSpec((K_TILE, width), lambda k, s: (tile_of(k, s), 0)),
            pl.BlockSpec((1, K_TILE), lambda k, s: (0, tile_of(k, s))),
            pl.BlockSpec((chain_w * rows_dev, 1), lambda k, s: (0, 0)),
        ],
        out_specs=pl.BlockSpec((chain_w * rows_dev, width), lambda k, s: (0, 0)),
    )
    return pl.pallas_call(
        masked_apply_kernel,
        grid_spec=grid_spec,
        out_shape=jax.ShapeDtypeStruct((chain_w * rows_dev, width), jnp.float32),
        compiler_params=pltpu.CompilerParams(
            dimension_semantics=("arbitrary",), vmem_limit_bytes=48 * 1024 * 1024
        ),
    )(span, env_rows, theta_all, sec_all.reshape(1, depth), sec_rows)


def per_device(theta, left_env, sector_ids, local_ops, edge_env):
    rows_dev = theta.shape[1]
    width = theta.shape[2]
    chain_w = left_env.shape[1]
    phys = local_ops.shape[2]
    cols = width // phys
    theta_loc = theta[0]
    env_loc = left_env[0]
    sec_all = sector_ids[0]
    ops_loc = local_ops[0]
    my_block = lax.axis_index("blk")
    row_start = my_block * rows_dev
    my_sec = lax.dynamic_slice_in_dim(sec_all, row_start, rows_dev, 0)
    theta_all = lax.all_gather(theta_loc, "blk", axis=0, tiled=True)
    applied = masked_apply(env_loc, theta_all, sec_all, my_sec)
    applied = applied.reshape(rows_dev, chain_w, phys, cols)
    acted = jnp.einsum("wpq,iwqc->ipc", ops_loc, applied, precision=lax.Precision.HIGH)
    theta_f = theta_loc.astype(jnp.float32).reshape(rows_dev, phys, cols)
    partial_intersection = jnp.einsum(
        "ipc,ipd->cd", theta_f, acted, precision=lax.Precision.HIGH
    )
    blk_peers = lax.axis_size("blk")
    intersection = grouped_sum(partial_intersection, "blk", (2, 4, blk_peers // 8))
    transfer = (
        intersection
        * jnp.sqrt(jnp.float32(cols))
        / jnp.sqrt(jnp.sum(intersection * intersection) + 1e-06)
    )
    received = gather_all(transfer, "sect")
    sect_no = lax.axis_index("sect")
    peers = lax.axis_size("sect")
    incoming = edge_env
    for step_no in range(peers - 1):
        factor = received[(sect_no - step_no) % peers]
        extended = matprod(incoming, factor)
        incoming = jnp.where(step_no < sect_no, extended, incoming)
    outgoing = matprod(incoming, transfer)
    result = jnp.einsum("ipc,cd->ipd", acted, incoming, precision=lax.Precision.HIGH)
    updated = result.reshape(1, rows_dev, width).astype(jnp.bfloat16)
    return (updated, outgoing[None])


def solution(mesh):
    placed = (
        P("sect", "blk", None),
        P("sect", None, "blk", None),
        P("sect", None),
        P("sect", None, None, None),
        P(),
    )
    return jax.shard_map(
        per_device,
        mesh=mesh,
        in_specs=placed,
        out_specs=(P("sect", "blk", None), P("sect", None, None)),
        check_vma=False,
    )
```

```python
import functools

import jax
import jax.numpy as jnp
from jax import lax
from jax.experimental import pallas as pl
from jax.experimental.pallas import tpu as pltpu
from jax.sharding import PartitionSpec as P

K_TILE = 256


def matprod(first, second):
    return jnp.dot(first, second, precision=lax.Precision.HIGH)


def grouped_sum(value, axis, sizes):
    peers = lax.axis_size(axis)
    stride = 1
    for size in sizes:
        total = value
        for shift in range(1, size):
            pairs = []
            for i in range(peers):
                digit = (i // stride) % size
                pairs.append((i, i + ((digit + shift) % size - digit) * stride))
            total = total + lax.ppermute(value, axis, pairs)
        value = total
        stride *= size
    return value


def gather_all(value, axis):
    peers = lax.axis_size(axis)
    parts = [value]
    for shift in range(1, peers):
        pairs = [(i, (i + shift) % peers) for i in range(peers)]
        parts.append(lax.ppermute(value, axis, pairs))
    return jnp.stack(parts)


def masked_apply_kernel(span_ref, env_ref, theta_ref, sec_j_ref, sec_i_ref, out_ref):
    step = pl.program_id(0)

    def product():
        env = env_ref[...]
        env = env.reshape(env.shape[0] * env.shape[1], env.shape[2])
        same = sec_i_ref[...] == sec_j_ref[...]
        masked = jnp.where(same, env, jnp.zeros_like(env))
        return jnp.dot(masked, theta_ref[...], preferred_element_type=jnp.float32)

    @pl.when(step == 0)
    def _():
        out_ref[...] = product()

    @pl.when((step > 0) & (span_ref[0] + step <= span_ref[1]))
    def _():
        out_ref[...] += product()


def masked_apply(env_loc, theta_all, sec_all, my_sec):
    chain_w, rows_dev, depth = env_loc.shape
    width = theta_all.shape[1]
    tiles = depth // K_TILE
    first = jnp.sum((sec_all < my_sec[0]).astype(jnp.int32))
    last = jnp.sum((sec_all <= my_sec[-1]).astype(jnp.int32)) - 1
    span = jnp.stack([first // K_TILE, last // K_TILE]).astype(jnp.int32)
    group = 16
    env_rows = jnp.transpose(env_loc, (1, 0, 2)).reshape(chain_w * rows_dev // group, group, depth)
    sec_rows = jnp.repeat(my_sec, chain_w).reshape(chain_w * rows_dev, 1)

    def tile_of(step, span_ref):
        return jnp.minimum(span_ref[0] + step, span_ref[1])

    grid_spec = pltpu.PrefetchScalarGridSpec(
        num_scalar_prefetch=1,
        grid=(tiles,),
        in_specs=[
            pl.BlockSpec((chain_w * rows_dev // group, group, K_TILE), lambda k, s: (0, 0, tile_of(k, s))),
            pl.BlockSpec((K_TILE, width), lambda k, s: (tile_of(k, s), 0)),
            pl.BlockSpec((1, K_TILE), lambda k, s: (0, tile_of(k, s))),
            pl.BlockSpec((chain_w * rows_dev, 1), lambda k, s: (0, 0)),
        ],
        out_specs=pl.BlockSpec((chain_w * rows_dev, width), lambda k, s: (0, 0)),
    )
    return pl.pallas_call(
        masked_apply_kernel,
        grid_spec=grid_spec,
        out_shape=jax.ShapeDtypeStruct((chain_w * rows_dev, width), jnp.float32),
        compiler_params=pltpu.CompilerParams(
            dimension_semantics=("arbitrary",), vmem_limit_bytes=48 * 1024 * 1024
        ),
    )(span, env_rows, theta_all, sec_all.reshape(1, depth), sec_rows)


def per_device(theta, left_env, sector_ids, local_ops, edge_env):
    rows_dev = theta.shape[1]
    width = theta.shape[2]
    chain_w = left_env.shape[1]
    phys = local_ops.shape[2]
    cols = width // phys
    theta_loc = theta[0]
    env_loc = left_env[0]
    sec_all = sector_ids[0]
    ops_loc = local_ops[0]
    my_block = lax.axis_index("blk")
    row_start = my_block * rows_dev
    my_sec = lax.dynamic_slice_in_dim(sec_all, row_start, rows_dev, 0)
    theta_all = lax.all_gather(theta_loc, "blk", axis=0, tiled=True)
    applied = masked_apply(env_loc, theta_all, sec_all, my_sec)
    applied = applied.reshape(rows_dev, chain_w, phys, cols)
    acted = jnp.einsum("wpq,iwqc->ipc", ops_loc, applied, precision=lax.Precision.HIGH)
    theta_f = theta_loc.astype(jnp.float32).reshape(rows_dev, phys, cols)
    partial_intersection = jnp.einsum(
        "ipc,ipd->cd", theta_f, acted, precision=lax.Precision.HIGH
    )
    blk_peers = lax.axis_size("blk")
    intersection = grouped_sum(partial_intersection, "blk", (2, 4, blk_peers // 8))
    transfer = (
        intersection
        * jnp.sqrt(jnp.float32(cols))
        / jnp.sqrt(jnp.sum(intersection * intersection) + 1e-06)
    )
    received = gather_all(transfer, "sect")
    sect_no = lax.axis_index("sect")
    peers = lax.axis_size("sect")
    incoming = edge_env
    for step_no in range(peers - 1):
        factor = received[(sect_no - step_no) % peers]
        extended = matprod(incoming, factor)
        incoming = jnp.where(step_no < sect_no, extended, incoming)
    outgoing = matprod(incoming, transfer)
    result = jnp.dot(acted.reshape(rows_dev * phys, cols), incoming, precision=lax.Precision.HIGH)
    updated = result.astype(jnp.bfloat16).reshape(1, rows_dev, width)
    return (updated, outgoing[None])


def solution(mesh):
    placed = (
        P("sect", "blk", None),
        P("sect", None, "blk", None),
        P("sect", None),
        P("sect", None, None, None),
        P(),
    )
    return jax.shard_map(
        per_device,
        mesh=mesh,
        in_specs=placed,
        out_specs=(P("sect", "blk", None), P("sect", None, None)),
        check_vma=False,
    )
```
